512 devices in a mesh: dp: 8 (over z_hi, core), dom: 64 (over x, z_lo, y).
Axes of the slice: x: 4, y: 4, z: 16 (z_hi: 4, z_lo: 4; z = z_hi * 4 + z_lo), core: 2. Of those that a mesh axis runs over, the one named last changes fastest.
Arguments:
- density: bfloat16 [8, 64, 512, 256], P('dp', None, 'dom'), may hold values from -6 to 6
- upstream: bfloat16 [8, 64, 512, 256], P('dp', None, 'dom'), may hold values from -6 to 6
- spectral_weight: float32 [2048, 64], P(('dp', 'dom')), may hold values from -0.5 to 0.5
- moment_one: float32 [2048, 64], P(('dp', 'dom')), may hold values from -128 to 128
- moment_two: float32 [2048, 64], P(('dp', 'dom')), may hold values from 256 to 4096
- skip_weight: bfloat16 [64, 64], replicated, may hold values from -0.75 to 0.75
- skip_bias: float32 [64], replicated, may hold values from -3 to 3
- mode_counts: int32 [8], replicated, may hold values from 8 to 16, as said below
Outputs:
- input_grad: bfloat16 [8, 64, 512, 256], P('dp', None, 'dom')
- new_weight: float32 [2048, 64], P(('dp', 'dom'))
- new_moment_one: float32 [2048, 64], P(('dp', 'dom'))
- new_moment_two: float32 [2048, 64], P(('dp', 'dom'))
The draws below stay inside these ranges and needn't reach their ends.
Inputs may be any that keep to these rules, and one draw needn't show every extreme that they name: `mode_counts`: some entry equals 16.
All inputs are finite; a program needn't handle non-finite values.
Results may differ from the reference program's by a relative error of at most 0.0053.
Values may be sent and summed in bfloat16 or wider, within the bound.
No kernel may reach another device: no remote copies, remote signals or barrier semaphores. Data moves between devices by JAX's collectives and lax.ppermute only.
A program may use at most 64 MiB of HBM per device.

```python
import math
import jax
import jax.numpy as jnp
from jax import lax

C = 64
MODES = 16
LINES = 256
STEP = 10
SAMPLES = 8
NX = 512


def draw_mode_counts(key, part):
    first_key, second_key = jax.random.split(jax.random.fold_in(key, 17))
    counts = jax.random.randint(first_key, (SAMPLES,), MODES // 2, MODES + 1, dtype=jnp.int32)
    chosen = jax.random.randint(second_key, (), 0, SAMPLES, dtype=jnp.int32)
    return jnp.where(jnp.arange(SAMPLES, dtype=jnp.int32) == chosen, MODES, counts).astype(jnp.int32)


def block_levels(rng, extent, shards, least, top_value):
    loudness = 1.0
    for dim, shards_of in shards:
        steps = jax.random.uniform(jax.random.fold_in(jax.random.fold_in(rng, 6), dim), (shards_of,), jnp.float32, least / len(shards), top_value / len(shards))
        loudness = loudness * jnp.repeat(jnp.exp(steps), extent[dim] // shards_of).reshape((-1,) + (1,) * (len(extent) - 1 - dim))
    return loudness


def bell_draw(own_key, dims, spread, limit, shards=(), kind=jnp.bfloat16):
    factor_of = block_levels(own_key, dims, shards, -0.22, 0.18) if shards else 1.0
    drawn = jax.random.normal(own_key, dims, jnp.float32) * spread * factor_of
    return jnp.minimum(jnp.maximum(drawn, -limit), limit).astype(kind)


def setup_inputs(seed: int = 0) -> dict:
    key_list = jax.random.split(jax.random.key(seed), 9)
    density = bell_draw(key_list[0], (SAMPLES, C, NX, LINES), 1.0, 6.0, ((0, 8), (2, 64)))
    upstream = bell_draw(key_list[1], (SAMPLES, C, NX, LINES), 1.0, 6.0, ((0, 8), (2, 64)))
    spectral_weight = bell_draw(key_list[2], (2 * MODES * C, C), (2 * C) ** -0.5, 0.5, ((0, 512),), jnp.float32)
    moment_one = bell_draw(key_list[3], (2 * MODES * C, C), (0.5 * (SAMPLES * LINES) ** 0.5), 128.0, ((0, 512),), jnp.float32)
    moment_two = jnp.clip(jnp.exp(math.log(4096.0) - 2.7725887 * jax.random.uniform(key_list[4], (2 * MODES * C, C), jnp.float32) ** block_levels(key_list[4], (2 * MODES * C, C), ((0, 512),), -0.2, 0.2)), 256.0, 4096.0)
    skip_weight = bell_draw(key_list[5], (C, C), C ** -0.5, 0.75)
    skip_bias = bell_draw(key_list[6], (C,), 0.5, 3.0, (), jnp.float32)
    mode_counts = draw_mode_counts(jax.random.fold_in(key_list[8], 71), 0)
    return {"density": density, "upstream": upstream, "spectral_weight": spectral_weight, "moment_one": moment_one, "moment_two": moment_two, "skip_weight": skip_weight, "skip_bias": skip_bias, "mode_counts": mode_counts}


learn_rate = 0.01
beta_first = 0.9
beta_second = 0.95
decay_rate = 0.1
epsilon = 1e-08

def upcast(values):
    return values.astype(jnp.float32)

def axis_parts(count_xdim):
    freq_list = jnp.arange(MODES, dtype=jnp.int32)
    cell_list = jnp.arange(count_xdim, dtype=jnp.int32)
    phases = jnp.mod(freq_list[:, None] * cell_list[None, :], count_xdim).astype(jnp.float32) / count_xdim
    angles = 2.0 * math.pi * phases
    scaling = 1.0 / math.sqrt(count_xdim)
    return ((jnp.cos(angles) * scaling).astype(jnp.bfloat16), (jnp.sin(angles) * scaling).astype(jnp.bfloat16))

def doubling_table():
    return jnp.where(jnp.arange(MODES, dtype=jnp.int32) > 0, 2.0, 1.0).astype(jnp.float32)

def gelu_slope(values):
    cumulative = 0.5 * (1.0 + lax.erf(values * 0.7071067811865476))
    bell_curve = jnp.exp(-0.5 * values * values) * 0.3989422804014327
    return cumulative + values * bell_curve

def reference(density, upstream, spectral_weight, moment_one, moment_two, skip_weight, skip_bias, mode_counts):
    cosines, sines = axis_parts(NX)
    cos_wide = upcast(cosines)
    sin_wide = upcast(sines)
    doubling = doubling_table()
    keep_modes = (jnp.arange(MODES, dtype=jnp.int32)[None, :] < mode_counts[:, None]).astype(jnp.float32)
    weight_low = spectral_weight.astype(jnp.bfloat16).reshape(2, MODES, C, C)
    weight_real = upcast(weight_low[0])
    weight_imag = upcast(weight_low[1])
    skip_wide = upcast(skip_weight)

    def one_sample(grad_sum, inputs):
        sample, cotangent, keep = inputs
        values = upcast(sample)
        spec_real = upcast(jnp.einsum('cxl,fx->lcf', values, cos_wide).astype(jnp.bfloat16))
        spec_imag = upcast((-jnp.einsum('cxl,fx->lcf', values, sin_wide)).astype(jnp.bfloat16))
        form = 'lcf,fco->lof'
        mixed_real = (jnp.einsum(form, spec_real, weight_real) - jnp.einsum(form, spec_imag, weight_imag)) * keep
        mixed_imag = (jnp.einsum(form, spec_imag, weight_real) + jnp.einsum(form, spec_real, weight_imag)) * keep
        mixed_real = upcast(mixed_real.astype(jnp.bfloat16)) * doubling
        mixed_imag = upcast(mixed_imag.astype(jnp.bfloat16)) * doubling
        back_rows = jnp.einsum('lof,fx->oxl', mixed_real, cos_wide) - jnp.einsum('lof,fx->oxl', mixed_imag, sin_wide)
        back_rows = lax.optimization_barrier(back_rows.astype(jnp.bfloat16))
        skip_part = jnp.einsum('oc,cxl->oxl', skip_wide, values)
        before = upcast(back_rows) + skip_part + skip_bias[:, None, None]
        gate_grad = (upcast(cotangent) * gelu_slope(before)).astype(jnp.bfloat16)
        gate_wide = upcast(gate_grad)
        scale = keep * doubling
        grad_real = upcast((jnp.einsum('oxl,fx->lof', gate_wide, cos_wide) * scale).astype(jnp.bfloat16))
        grad_imag = upcast((-jnp.einsum('oxl,fx->lof', gate_wide, sin_wide) * scale).astype(jnp.bfloat16))
        outer = 'lof,lcf->fco'
        part_real = jnp.einsum(outer, grad_real, spec_real) + jnp.einsum(outer, grad_imag, spec_imag)
        part_imag = jnp.einsum(outer, grad_imag, spec_real) - jnp.einsum(outer, grad_real, spec_imag)
        grad_sum = grad_sum + jnp.stack([part_real, part_imag], 0)
        inner = 'fco,lof->lcf'
        input_real = jnp.einsum(inner, weight_real, grad_real) + jnp.einsum(inner, weight_imag, grad_imag)
        input_imag = jnp.einsum(inner, weight_real, grad_imag) - jnp.einsum(inner, weight_imag, grad_real)
        input_real = upcast(input_real.astype(jnp.bfloat16))
        input_imag = upcast(input_imag.astype(jnp.bfloat16))
        input_rows = jnp.einsum('lcf,fx->cxl', input_real, cos_wide) - jnp.einsum('lcf,fx->cxl', input_imag, sin_wide)
        input_rows = lax.optimization_barrier(input_rows.astype(jnp.bfloat16))
        skip_back = jnp.einsum('oc,oxl->cxl', skip_wide, gate_wide)
        return (grad_sum, (upcast(input_rows) + skip_back).astype(jnp.bfloat16))
    start_sum = jnp.zeros((2, MODES, C, C), jnp.float32)
    grad_whole, input_grad = lax.scan(one_sample, start_sum, (density, upstream, keep_modes))
    weight_grad = grad_whole.reshape(2 * MODES * C, C)
    new_moment_one = beta_first * moment_one + (1.0 - beta_first) * weight_grad
    new_moment_two = beta_second * moment_two + (1.0 - beta_second) * weight_grad * weight_grad
    first_hat = new_moment_one / (1.0 - beta_first ** STEP)
    second_hat = new_moment_two / (1.0 - beta_second ** STEP)
    new_weight = spectral_weight - learn_rate * (first_hat / (jnp.sqrt(second_hat) + epsilon) + decay_rate * spectral_weight)
    return (input_grad, new_weight, new_moment_one, new_moment_two)
```

```python
import math

import jax
import jax.numpy as jnp
from jax import lax
from jax.sharding import PartitionSpec as P

MODES = 16
STEP = 10


learn_rate = 0.01
beta_first = 0.9
beta_second = 0.95
decay_rate = 0.1
epsilon = 1e-08


def joined_along(tiles, dim):
    dims = list(tiles.shape[1:])
    dims[dim] *= tiles.shape[0]
    return jnp.moveaxis(tiles, 0, dim).reshape(dims)


def copy_for_each(shard, axis):
    copies = jnp.broadcast_to(shard, (lax.axis_size(axis), *shard.shape))
    return lax.all_to_all(copies, axis, split_axis=0, concat_axis=0, tiled=True)


def collect(shard, axis, dim):
    return joined_along(copy_for_each(shard, axis), dim)


def in_one_piece(arrays, axis, split_dim, concat_dim, along):
    both = jnp.concatenate(arrays, axis=along)
    result, at, done = (
        lax.all_to_all(both, axis, split_axis=split_dim, concat_axis=concat_dim, tiled=True),
        0,
        [],
    )
    for a in arrays:
        done.append(lax.slice_in_dim(result, at, at + a.shape[along], axis=along))
        at += a.shape[along]
    return tuple(done)


def split_up(shard, dim, length):
    dims = shard.shape
    tiles = shard.reshape(*dims[:dim], length, dims[dim] // length, *dims[dim + 1 :])
    return jnp.moveaxis(tiles, dim, 0)


def sum_at_owner(shard, axis, dim):
    tiles = split_up(shard, dim, lax.axis_size(axis))
    arrived = lax.all_to_all(tiles, axis, split_axis=0, concat_axis=0, tiled=True)
    return arrived.astype(jnp.float32).sum(axis=0)


def summed_on_arrival(shard, axis, dim):
    length = lax.axis_size(axis)
    tiles = lax.all_to_all(split_up(shard, dim, length), axis, 0, 0, tiled=True)
    return jnp.sum(tiles, axis=0)


def axis_parts(count_xdim):
    freq_list = jnp.arange(MODES, dtype=jnp.int32)
    cell_list = jnp.arange(count_xdim, dtype=jnp.int32)
    phases = (
        jnp.mod(freq_list[:, None] * cell_list[None, :], count_xdim).astype(jnp.float32)
        / count_xdim
    )
    angles = 2.0 * math.pi * phases
    scaling = 1.0 / math.sqrt(count_xdim)
    return (
        (jnp.cos(angles) * scaling).astype(jnp.bfloat16),
        (jnp.sin(angles) * scaling).astype(jnp.bfloat16),
    )


def doubling_table():
    return jnp.where(jnp.arange(MODES, dtype=jnp.int32) > 0, 2.0, 1.0).astype(jnp.float32)


def gelu_slope(values):
    cumulative = 0.5 * (1.0 + lax.erf(values * 0.7071067811865476))
    bell_curve = jnp.exp(-0.5 * values * values) * 0.3989422804014327
    return cumulative + values * bell_curve


def forward_parts(field, cosines, sines):
    real_part = jnp.einsum("scxl,fx->slcf", field, cosines, preferred_element_type=jnp.float32)
    imag_part = -jnp.einsum("scxl,fx->slcf", field, sines, preferred_element_type=jnp.float32)
    return (real_part, imag_part)


def inverse_cells(values_real, values_imag, cosines, sines):
    first = jnp.einsum("slcf,fx->scxl", values_real, cosines, preferred_element_type=jnp.float32)
    second = jnp.einsum("slcf,fx->scxl", values_imag, sines, preferred_element_type=jnp.float32)
    return (first - second).astype(jnp.bfloat16)


def on_device(
    density, upstream, spectral_weight, moment_one, moment_two, skip_weight, skip_bias, mode_counts
):
    samples, channels, slab_rows, line_count = density.shape
    count_xdim = slab_rows * lax.axis_size("dom")
    cosines, sines = axis_parts(count_xdim)
    doubling = doubling_table()
    doubling_low = doubling.astype(jnp.bfloat16)
    counts_here = lax.dynamic_slice_in_dim(mode_counts, lax.axis_index("dp") * samples, samples, 0)
    keep_modes = (jnp.arange(MODES, dtype=jnp.int32)[None, :] < counts_here[:, None]).astype(
        jnp.float32
    )
    keep_wide = keep_modes[:, None, None, :]
    weight_short = spectral_weight.astype(jnp.bfloat16)
    weight_low = lax.all_gather(weight_short, ("dp", "dom"), axis=0, tiled=True)
    weight_low = weight_low.reshape(2, MODES, channels, channels)
    weight_real = weight_low[0]
    weight_imag = weight_low[1]
    density_lines, upstream_lines = in_one_piece((density, upstream), "dom", 3, 2, 0)
    real_part, imag_part = forward_parts(density_lines, cosines, sines)
    spec_real = real_part.astype(jnp.bfloat16)
    spec_imag = imag_part.astype(jnp.bfloat16)
    form = "slcf,fco->slof"
    mixed_real = jnp.einsum(
        form, spec_real, weight_real, preferred_element_type=jnp.float32
    ) - jnp.einsum(form, spec_imag, weight_imag, preferred_element_type=jnp.float32)
    mixed_imag = jnp.einsum(
        form, spec_imag, weight_real, preferred_element_type=jnp.float32
    ) + jnp.einsum(form, spec_real, weight_imag, preferred_element_type=jnp.float32)
    mixed_real = (mixed_real * keep_wide).astype(jnp.bfloat16) * doubling_low
    mixed_imag = (mixed_imag * keep_wide).astype(jnp.bfloat16) * doubling_low
    back_lines = inverse_cells(mixed_real, mixed_imag, cosines, sines)
    back_rows = lax.optimization_barrier(back_lines)
    skip_part = jnp.einsum(
        "oc,scxl->soxl", skip_weight, density_lines, preferred_element_type=jnp.float32
    )
    before = back_rows.astype(jnp.float32) + skip_part + skip_bias[None, :, None, None]
    gate_lines = (upstream_lines.astype(jnp.float32) * gelu_slope(before)).astype(jnp.bfloat16)
    grad_real, grad_imag = forward_parts(gate_lines, cosines, sines)
    scale = keep_wide * doubling
    grad_real = (grad_real * scale).astype(jnp.bfloat16)
    grad_imag = (grad_imag * scale).astype(jnp.bfloat16)
    outer = "slof,slcf->fco"
    part_real = jnp.einsum(
        outer, grad_real, spec_real, preferred_element_type=jnp.float32
    ) + jnp.einsum(outer, grad_imag, spec_imag, preferred_element_type=jnp.float32)
    part_imag = jnp.einsum(
        outer, grad_imag, spec_real, preferred_element_type=jnp.float32
    ) - jnp.einsum(outer, grad_real, spec_imag, preferred_element_type=jnp.float32)
    grad_local = jnp.stack([part_real, part_imag], 0).reshape(2 * MODES * channels, channels)
    weight_grad = lax.psum_scatter(grad_local, ("dp", "dom"), scatter_dimension=0, tiled=True)
    inner = "fco,slof->slcf"
    input_real = jnp.einsum(
        inner, weight_real, grad_real, preferred_element_type=jnp.float32
    ) + jnp.einsum(inner, weight_imag, grad_imag, preferred_element_type=jnp.float32)
    input_imag = jnp.einsum(
        inner, weight_real, grad_imag, preferred_element_type=jnp.float32
    ) - jnp.einsum(inner, weight_imag, grad_real, preferred_element_type=jnp.float32)
    input_lines = inverse_cells(
        input_real.astype(jnp.bfloat16), input_imag.astype(jnp.bfloat16), cosines, sines
    )
    input_rows = lax.optimization_barrier(input_lines)
    skip_back = jnp.einsum(
        "oc,soxl->scxl", skip_weight, gate_lines, preferred_element_type=jnp.float32
    )
    grad_lines = (input_rows.astype(jnp.float32) + skip_back).astype(jnp.bfloat16)
    input_grad = lax.all_to_all(grad_lines, "dom", split_axis=2, concat_axis=3, tiled=True)
    new_moment_one = beta_first * moment_one + (1.0 - beta_first) * weight_grad
    new_moment_two = beta_second * moment_two + (1.0 - beta_second) * weight_grad * weight_grad
    first_hat = new_moment_one / (1.0 - beta_first**STEP)
    second_hat = new_moment_two / (1.0 - beta_second**STEP)
    new_weight = spectral_weight - learn_rate * (
        first_hat / (jnp.sqrt(second_hat) + epsilon) + decay_rate * spectral_weight
    )
    return (input_grad, new_weight, new_moment_one, new_moment_two)


def solution(mesh):
    placed = (
        P("dp", None, "dom", None),
        P("dp", None, "dom", None),
        P(("dp", "dom"), None),
        P(("dp", "dom"), None),
        P(("dp", "dom"), None),
        P(),
        P(),
        P(),
    )
    return jax.shard_map(
        on_device,
        mesh=mesh,
        in_specs=placed,
        out_specs=(
            P("dp", None, "dom", None),
            P(("dp", "dom"), None),
            P(("dp", "dom"), None),
            P(("dp", "dom"), None),
        ),
        check_vma=False,
    )
```

```python
import math

import jax
import jax.numpy as jnp
from jax import lax
from jax.sharding import PartitionSpec as P

MODES = 16
STEP = 10


learn_rate = 0.01
beta_first = 0.9
beta_second = 0.95
decay_rate = 0.1
epsilon = 1e-08


def joined_along(tiles, dim):
    dims = list(tiles.shape[1:])
    dims[dim] *= tiles.shape[0]
    return jnp.moveaxis(tiles, 0, dim).reshape(dims)


def copy_for_each(shard, axis):
    copies = jnp.broadcast_to(shard, (lax.axis_size(axis), *shard.shape))
    return lax.all_to_all(copies, axis, split_axis=0, concat_axis=0, tiled=True)


def collect(shard, axis, dim):
    return joined_along(copy_for_each(shard, axis), dim)


def in_one_piece(arrays, axis, split_dim, concat_dim, along):
    both = jnp.concatenate(arrays, axis=along)
    result, at, done = (
        lax.all_to_all(both, axis, split_axis=split_dim, concat_axis=concat_dim, tiled=True),
        0,
        [],
    )
    for a in arrays:
        done.append(lax.slice_in_dim(result, at, at + a.shape[along], axis=along))
        at += a.shape[along]
    return tuple(done)


def split_up(shard, dim, length):
    dims = shard.shape
    tiles = shard.reshape(*dims[:dim], length, dims[dim] // length, *dims[dim + 1 :])
    return jnp.moveaxis(tiles, dim, 0)


def sum_at_owner(shard, axis, dim):
    tiles = split_up(shard, dim, lax.axis_size(axis))
    arrived = lax.all_to_all(tiles, axis, split_axis=0, concat_axis=0, tiled=True)
    return arrived.astype(jnp.float32).sum(axis=0)


def summed_on_arrival(shard, axis, dim):
    length = lax.axis_size(axis)
    tiles = lax.all_to_all(split_up(shard, dim, length), axis, 0, 0, tiled=True)
    return jnp.sum(tiles, axis=0)


def axis_parts(count_xdim):
    freq_list = jnp.arange(MODES, dtype=jnp.int32)
    cell_list = jnp.arange(count_xdim, dtype=jnp.int32)
    phases = (
        jnp.mod(freq_list[:, None] * cell_list[None, :], count_xdim).astype(jnp.float32)
        / count_xdim
    )
    angles = 2.0 * math.pi * phases
    scaling = 1.0 / math.sqrt(count_xdim)
    return (
        (jnp.cos(angles) * scaling).astype(jnp.bfloat16),
        (jnp.sin(angles) * scaling).astype(jnp.bfloat16),
    )


def doubling_table():
    return jnp.where(jnp.arange(MODES, dtype=jnp.int32) > 0, 2.0, 1.0).astype(jnp.float32)


def gelu_slope(values):
    cumulative = 0.5 * (1.0 + lax.erf(values * 0.7071067811865476))
    bell_curve = jnp.exp(-0.5 * values * values) * 0.3989422804014327
    return cumulative + values * bell_curve


def forward_parts(field, cosines, sines):
    real_part = jnp.einsum("scxl,fx->slcf", field, cosines, preferred_element_type=jnp.float32)
    imag_part = -jnp.einsum("scxl,fx->slcf", field, sines, preferred_element_type=jnp.float32)
    return (real_part, imag_part)


def inverse_cells(values_real, values_imag, cosines, sines):
    first = jnp.einsum("slcf,fx->scxl", values_real, cosines, preferred_element_type=jnp.float32)
    second = jnp.einsum("slcf,fx->scxl", values_imag, sines, preferred_element_type=jnp.float32)
    return (first - second).astype(jnp.bfloat16)


def gather_over_dp(rows):
    count = lax.axis_size("dp")
    pairs = lambda k: [(i, (i + k) % count) for i in range(count)]
    here = lax.axis_index("dp")
    pieces = [rows] + [lax.ppermute(rows, "dp", pairs(k)) for k in range(1, count)]
    stacked = jnp.stack(pieces, 0)
    order = (here - jnp.arange(count)) % count
    return jnp.take(stacked, order, axis=0)


def scatter_sum_over_dp(blocks):
    count = lax.axis_size("dp")
    pairs = lambda k: [(i, (i + k) % count) for i in range(count)]
    here = lax.axis_index("dp")
    total = lax.dynamic_index_in_dim(blocks, here, 0, keepdims=False)
    for k in range(1, count):
        sent = lax.dynamic_index_in_dim(blocks, (here + k) % count, 0, keepdims=False)
        total = total + lax.ppermute(sent, "dp", pairs(k))
    return total


def on_device(
    density, upstream, spectral_weight, moment_one, moment_two, skip_weight, skip_bias, mode_counts
):
    samples, channels, slab_rows, line_count = density.shape
    slabs = lax.axis_size("dom")
    groups = lax.axis_size("dp")
    count_xdim = slab_rows * slabs
    lines_here = line_count // slabs
    cosines, sines = axis_parts(count_xdim)
    doubling = doubling_table()
    doubling_low = doubling.astype(jnp.bfloat16)
    counts_here = lax.dynamic_slice_in_dim(mode_counts, lax.axis_index("dp") * samples, samples, 0)
    keep_modes = (jnp.arange(MODES, dtype=jnp.int32)[None, :] < counts_here[:, None]).astype(
        jnp.float32
    )
    keep_wide = keep_modes[:, None, None, :]
    rows_here = spectral_weight.shape[0]
    weight_short = spectral_weight.astype(jnp.bfloat16)
    group_rows = gather_over_dp(weight_short).reshape(1, groups * rows_here * channels)

    def to_tiles(field):
        tiles = field.reshape(samples, channels, slab_rows, slabs, lines_here)
        return jnp.moveaxis(tiles, 3, 0).reshape(slabs, -1)

    def from_tiles(tiles):
        field = tiles.reshape(slabs, samples, channels, slab_rows, lines_here)
        return jnp.moveaxis(field, 0, 2).reshape(samples, channels, count_xdim, lines_here)

    size = samples * channels * slab_rows * lines_here
    outgoing = jnp.concatenate(
        [to_tiles(density), to_tiles(upstream), jnp.broadcast_to(group_rows, (slabs, group_rows.shape[1]))],
        axis=1,
    )
    arrived = lax.all_to_all(outgoing, "dom", 0, 0, tiled=True)
    density_lines = from_tiles(arrived[:, :size])
    upstream_lines = from_tiles(arrived[:, size : 2 * size])
    weight_rows = arrived[:, 2 * size :].reshape(slabs, groups, rows_here, channels)
    weight_low = jnp.moveaxis(weight_rows, 0, 1).reshape(2, MODES, channels, channels)
    weight_real = weight_low[0]
    weight_imag = weight_low[1]
    real_part, imag_part = forward_parts(density_lines, cosines, sines)
    spec_real = real_part.astype(jnp.bfloat16)
    spec_imag = imag_part.astype(jnp.bfloat16)
    form = "slcf,fco->slof"
    mixed_real = jnp.einsum(
        form, spec_real, weight_real, preferred_element_type=jnp.float32
    ) - jnp.einsum(form, spec_imag, weight_imag, preferred_element_type=jnp.float32)
    mixed_imag = jnp.einsum(
        form, spec_imag, weight_real, preferred_element_type=jnp.float32
    ) + jnp.einsum(form, spec_real, weight_imag, preferred_element_type=jnp.float32)
    mixed_real = (mixed_real * keep_wide).astype(jnp.bfloat16) * doubling_low
    mixed_imag = (mixed_imag * keep_wide).astype(jnp.bfloat16) * doubling_low
    back_lines = inverse_cells(mixed_real, mixed_imag, cosines, sines)
    back_rows = lax.optimization_barrier(back_lines)
    skip_part = jnp.einsum(
        "oc,scxl->soxl", skip_weight, density_lines, preferred_element_type=jnp.float32
    )
    before = back_rows.astype(jnp.float32) + skip_part + skip_bias[None, :, None, None]
    gate_lines = (upstream_lines.astype(jnp.float32) * gelu_slope(before)).astype(jnp.bfloat16)
    grad_real, grad_imag = forward_parts(gate_lines, cosines, sines)
    scale = keep_wide * doubling
    grad_real = (grad_real * scale).astype(jnp.bfloat16)
    grad_imag = (grad_imag * scale).astype(jnp.bfloat16)
    outer = "slof,slcf->fco"
    part_real = jnp.einsum(
        outer, grad_real, spec_real, preferred_element_type=jnp.float32
    ) + jnp.einsum(outer, grad_imag, spec_imag, preferred_element_type=jnp.float32)
    part_imag = jnp.einsum(
        outer, grad_imag, spec_real, preferred_element_type=jnp.float32
    ) - jnp.einsum(outer, grad_real, spec_imag, preferred_element_type=jnp.float32)
    grad_local = jnp.stack([part_real, part_imag], 0).reshape(groups, slabs, rows_here, channels)
    grad_tiles = jnp.moveaxis(grad_local.astype(jnp.bfloat16), 1, 0).reshape(slabs, -1)
    inner = "fco,slof->slcf"
    input_real = jnp.einsum(
        inner, weight_real, grad_real, preferred_element_type=jnp.float32
    ) + jnp.einsum(inner, weight_imag, grad_imag, preferred_element_type=jnp.float32)
    input_imag = jnp.einsum(
        inner, weight_real, grad_imag, preferred_element_type=jnp.float32
    ) - jnp.einsum(inner, weight_imag, grad_real, preferred_element_type=jnp.float32)
    input_lines = inverse_cells(
        input_real.astype(jnp.bfloat16), input_imag.astype(jnp.bfloat16), cosines, sines
    )
    input_rows = lax.optimization_barrier(input_lines)
    skip_back = jnp.einsum(
        "oc,soxl->scxl", skip_weight, gate_lines, preferred_element_type=jnp.float32
    )
    grad_lines = (input_rows.astype(jnp.float32) + skip_back).astype(jnp.bfloat16)
    line_tiles = grad_lines.reshape(samples, channels, slabs, slab_rows, lines_here)
    line_tiles = jnp.moveaxis(line_tiles, 2, 0).reshape(slabs, -1)
    returned = lax.all_to_all(
        jnp.concatenate([line_tiles, grad_tiles], axis=1), "dom", 0, 0, tiled=True
    )
    input_grad = returned[:, :size].reshape(slabs, samples, channels, slab_rows, lines_here)
    input_grad = jnp.moveaxis(input_grad, 0, 3).reshape(samples, channels, slab_rows, line_count)
    group_grad = returned[:, size:].astype(jnp.float32).reshape(slabs, groups, rows_here, channels)
    weight_grad = scatter_sum_over_dp(group_grad.sum(axis=0))
    new_moment_one = beta_first * moment_one + (1.0 - beta_first) * weight_grad
    new_moment_two = beta_second * moment_two + (1.0 - beta_second) * weight_grad * weight_grad
    first_hat = new_moment_one / (1.0 - beta_first**STEP)
    second_hat = new_moment_two / (1.0 - beta_second**STEP)
    new_weight = spectral_weight - learn_rate * (
        first_hat / (jnp.sqrt(second_hat) + epsilon) + decay_rate * spectral_weight
    )
    return (input_grad, new_weight, new_moment_one, new_moment_two)


def solution(mesh):
    placed = (
        P("dp", None, "dom", None),
        P("dp", None, "dom", None),
        P(("dp", "dom"), None),
        P(("dp", "dom"), None),
        P(("dp", "dom"), None),
        P(),
        P(),
        P(),
    )
    return jax.shard_map(
        on_device,
        mesh=mesh,
        in_specs=placed,
        out_specs=(
            P("dp", None, "dom", None),
            P(("dp", "dom"), None),
            P(("dp", "dom"), None),
            P(("dp", "dom"), None),
        ),
        check_vma=False,
    )
```

```python
import math

import jax
import jax.numpy as jnp
from jax import lax
from jax.sharding import PartitionSpec as P

MODES = 16
STEP = 10


learn_rate = 0.01
beta_first = 0.9
beta_second = 0.95
decay_rate = 0.1
epsilon = 1e-08


def joined_along(tiles, dim):
    dims = list(tiles.shape[1:])
    dims[dim] *= tiles.shape[0]
    return jnp.moveaxis(tiles, 0, dim).reshape(dims)


def copy_for_each(shard, axis):
    copies = jnp.broadcast_to(shard, (lax.axis_size(axis), *shard.shape))
    return lax.all_to_all(copies, axis, split_axis=0, concat_axis=0, tiled=True)


def collect(shard, axis, dim):
    return joined_along(copy_for_each(shard, axis), dim)


def in_one_piece(arrays, axis, split_dim, concat_dim, along):
    both = jnp.concatenate(arrays, axis=along)
    result, at, done = (
        lax.all_to_all(both, axis, split_axis=split_dim, concat_axis=concat_dim, tiled=True),
        0,
        [],
    )
    for a in arrays:
        done.append(lax.slice_in_dim(result, at, at + a.shape[along], axis=along))
        at += a.shape[along]
    return tuple(done)


def split_up(shard, dim, length):
    dims = shard.shape
    tiles = shard.reshape(*dims[:dim], length, dims[dim] // length, *dims[dim + 1 :])
    return jnp.moveaxis(tiles, dim, 0)


def sum_at_owner(shard, axis, dim):
    tiles = split_up(shard, dim, lax.axis_size(axis))
    arrived = lax.all_to_all(tiles, axis, split_axis=0, concat_axis=0, tiled=True)
    return arrived.astype(jnp.float32).sum(axis=0)


def summed_on_arrival(shard, axis, dim):
    length = lax.axis_size(axis)
    tiles = lax.all_to_all(split_up(shard, dim, length), axis, 0, 0, tiled=True)
    return jnp.sum(tiles, axis=0)


def axis_parts(count_xdim):
    freq_list = jnp.arange(MODES, dtype=jnp.int32)
    cell_list = jnp.arange(count_xdim, dtype=jnp.int32)
    phases = (
        jnp.mod(freq_list[:, None] * cell_list[None, :], count_xdim).astype(jnp.float32)
        / count_xdim
    )
    angles = 2.0 * math.pi * phases
    scaling = 1.0 / math.sqrt(count_xdim)
    return (
        (jnp.cos(angles) * scaling).astype(jnp.bfloat16),
        (jnp.sin(angles) * scaling).astype(jnp.bfloat16),
    )


def doubling_table():
    return jnp.where(jnp.arange(MODES, dtype=jnp.int32) > 0, 2.0, 1.0).astype(jnp.float32)


def gelu_slope(values):
    cumulative = 0.5 * (1.0 + lax.erf(values * 0.7071067811865476))
    bell_curve = jnp.exp(-0.5 * values * values) * 0.3989422804014327
    return cumulative + values * bell_curve


def forward_parts(field, cosines, sines):
    real_part = jnp.einsum("scxl,fx->slcf", field, cosines, preferred_element_type=jnp.float32)
    imag_part = -jnp.einsum("scxl,fx->slcf", field, sines, preferred_element_type=jnp.float32)
    return (real_part, imag_part)


def inverse_cells(values_real, values_imag, cosines, sines):
    first = jnp.einsum("slcf,fx->scxl", values_real, cosines, preferred_element_type=jnp.float32)
    second = jnp.einsum("slcf,fx->scxl", values_imag, sines, preferred_element_type=jnp.float32)
    return (first - second).astype(jnp.bfloat16)


def on_device(
    density, upstream, spectral_weight, moment_one, moment_two, skip_weight, skip_bias, mode_counts
):
    samples, channels, slab_rows, line_count = density.shape
    count_xdim = slab_rows * lax.axis_size("dom")
    cosines, sines = axis_parts(count_xdim)
    doubling = doubling_table()
    doubling_low = doubling.astype(jnp.bfloat16)
    counts_here = lax.dynamic_slice_in_dim(mode_counts, lax.axis_index("dp") * samples, samples, 0)
    keep_modes = (jnp.arange(MODES, dtype=jnp.int32)[None, :] < counts_here[:, None]).astype(
        jnp.float32
    )
    keep_wide = keep_modes[:, None, None, :]
    weight_short = spectral_weight.astype(jnp.bfloat16)
    group_low = collect(weight_short, "dom", 0)
    weight_low = lax.all_gather(group_low, "dp", axis=0, tiled=True)
    weight_low = weight_low.reshape(2, MODES, channels, channels)
    weight_real = weight_low[0]
    weight_imag = weight_low[1]
    density_lines, upstream_lines = in_one_piece((density, upstream), "dom", 3, 2, 0)
    real_part, imag_part = forward_parts(density_lines, cosines, sines)
    spec_real = real_part.astype(jnp.bfloat16)
    spec_imag = imag_part.astype(jnp.bfloat16)
    form = "slcf,fco->slof"
    mixed_real = jnp.einsum(
        form, spec_real, weight_real, preferred_element_type=jnp.float32
    ) - jnp.einsum(form, spec_imag, weight_imag, preferred_element_type=jnp.float32)
    mixed_imag = jnp.einsum(
        form, spec_imag, weight_real, preferred_element_type=jnp.float32
    ) + jnp.einsum(form, spec_real, weight_imag, preferred_element_type=jnp.float32)
    mixed_real = (mixed_real * keep_wide).astype(jnp.bfloat16) * doubling_low
    mixed_imag = (mixed_imag * keep_wide).astype(jnp.bfloat16) * doubling_low
    back_lines = inverse_cells(mixed_real, mixed_imag, cosines, sines)
    back_rows = lax.optimization_barrier(back_lines)
    skip_part = jnp.einsum(
        "oc,scxl->soxl", skip_weight, density_lines, preferred_element_type=jnp.float32
    )
    before = back_rows.astype(jnp.float32) + skip_part + skip_bias[None, :, None, None]
    gate_lines = (upstream_lines.astype(jnp.float32) * gelu_slope(before)).astype(jnp.bfloat16)
    grad_real, grad_imag = forward_parts(gate_lines, cosines, sines)
    scale = keep_wide * doubling
    grad_real = (grad_real * scale).astype(jnp.bfloat16)
    grad_imag = (grad_imag * scale).astype(jnp.bfloat16)
    outer = "slof,slcf->fco"
    part_real = jnp.einsum(
        outer, grad_real, spec_real, preferred_element_type=jnp.float32
    ) + jnp.einsum(outer, grad_imag, spec_imag, preferred_element_type=jnp.float32)
    part_imag = jnp.einsum(
        outer, grad_imag, spec_real, preferred_element_type=jnp.float32
    ) - jnp.einsum(outer, grad_real, spec_imag, preferred_element_type=jnp.float32)
    groups = lax.axis_size("dp")
    slabs = lax.axis_size("dom")
    rows_here = spectral_weight.shape[0]
    grad_local = jnp.stack([part_real, part_imag], 0).astype(jnp.bfloat16)
    grad_tiles = jnp.moveaxis(grad_local.reshape(groups, slabs, rows_here, channels), 1, 0)
    inner = "fco,slof->slcf"
    input_real = jnp.einsum(
        inner, weight_real, grad_real, preferred_element_type=jnp.float32
    ) + jnp.einsum(inner, weight_imag, grad_imag, preferred_element_type=jnp.float32)
    input_imag = jnp.einsum(
        inner, weight_real, grad_imag, preferred_element_type=jnp.float32
    ) - jnp.einsum(inner, weight_imag, grad_real, preferred_element_type=jnp.float32)
    input_lines = inverse_cells(
        input_real.astype(jnp.bfloat16), input_imag.astype(jnp.bfloat16), cosines, sines
    )
    input_rows = lax.optimization_barrier(input_lines)
    skip_back = jnp.einsum(
        "oc,soxl->scxl", skip_weight, gate_lines, preferred_element_type=jnp.float32
    )
    grad_lines = (input_rows.astype(jnp.float32) + skip_back).astype(jnp.bfloat16)
    lines_here = grad_lines.shape[3]
    line_tiles = grad_lines.reshape(samples, channels, slabs, slab_rows, lines_here)
    line_tiles = jnp.moveaxis(line_tiles, 2, 0).reshape(slabs, -1)
    size = line_tiles.shape[1]
    returned = lax.all_to_all(
        jnp.concatenate([line_tiles, grad_tiles.reshape(slabs, -1)], axis=1),
        "dom",
        0,
        0,
        tiled=True,
    )
    input_grad = returned[:, :size].reshape(slabs, samples, channels, slab_rows, lines_here)
    input_grad = jnp.moveaxis(input_grad, 0, 3).reshape(samples, channels, slab_rows, -1)
    group_grad = returned[:, size:].astype(jnp.float32).reshape(slabs, groups, rows_here, channels)
    group_grad = group_grad.sum(axis=0)
    every_group = lax.all_gather(group_grad, "dp", axis=0, tiled=False)
    mine = lax.dynamic_index_in_dim(every_group, lax.axis_index("dp"), 1, keepdims=False)
    weight_grad = mine.sum(axis=0)
    new_moment_one = beta_first * moment_one + (1.0 - beta_first) * weight_grad
    new_moment_two = beta_second * moment_two + (1.0 - beta_second) * weight_grad * weight_grad
    first_hat = new_moment_one / (1.0 - beta_first**STEP)
    second_hat = new_moment_two / (1.0 - beta_second**STEP)
    new_weight = spectral_weight - learn_rate * (
        first_hat / (jnp.sqrt(second_hat) + epsilon) + decay_rate * spectral_weight
    )
    return (input_grad, new_weight, new_moment_one, new_moment_two)


def solution(mesh):
    placed = (
        P("dp", None, "dom", None),
        P("dp", None, "dom", None),
        P(("dp", "dom"), None),
        P(("dp", "dom"), None),
        P(("dp", "dom"), None),
        P(),
        P(),
        P(),
    )
    return jax.shard_map(
        on_device,
        mesh=mesh,
        in_specs=placed,
        out_specs=(
            P("dp", None, "dom", None),
            P(("dp", "dom"), None),
            P(("dp", "dom"), None),
            P(("dp", "dom"), None),
        ),
        check_vma=False,
    )
```

```python
import math

import jax
import jax.numpy as jnp
from jax import lax
from jax.sharding import PartitionSpec as P

MODES = 16
STEP = 10


learn_rate = 0.01
beta_first = 0.9
beta_second = 0.95
decay_rate = 0.1
epsilon = 1e-08


def joined_along(tiles, dim):
    dims = list(tiles.shape[1:])
    dims[dim] *= tiles.shape[0]
    return jnp.moveaxis(tiles, 0, dim).reshape(dims)


def copy_for_each(shard, axis):
    copies = jnp.broadcast_to(shard, (lax.axis_size(axis), *shard.shape))
    return lax.all_to_all(copies, axis, split_axis=0, concat_axis=0, tiled=True)


def collect(shard, axis, dim):
    return joined_along(copy_for_each(shard, axis), dim)


def in_one_piece(arrays, axis, split_dim, concat_dim, along):
    both = jnp.concatenate(arrays, axis=along)
    result, at, done = (
        lax.all_to_all(both, axis, split_axis=split_dim, concat_axis=concat_dim, tiled=True),
        0,
        [],
    )
    for a in arrays:
        done.append(lax.slice_in_dim(result, at, at + a.shape[along], axis=along))
        at += a.shape[along]
    return tuple(done)


def split_up(shard, dim, length):
    dims = shard.shape
    tiles = shard.reshape(*dims[:dim], length, dims[dim] // length, *dims[dim + 1 :])
    return jnp.moveaxis(tiles, dim, 0)


def sum_at_owner(shard, axis, dim):
    tiles = split_up(shard, dim, lax.axis_size(axis))
    arrived = lax.all_to_all(tiles, axis, split_axis=0, concat_axis=0, tiled=True)
    return arrived.astype(jnp.float32).sum(axis=0)


def summed_on_arrival(shard, axis, dim):
    length = lax.axis_size(axis)
    tiles = lax.all_to_all(split_up(shard, dim, length), axis, 0, 0, tiled=True)
    return jnp.sum(tiles, axis=0)


def axis_parts(count_xdim):
    freq_list = jnp.arange(MODES, dtype=jnp.int32)
    cell_list = jnp.arange(count_xdim, dtype=jnp.int32)
    phases = (
        jnp.mod(freq_list[:, None] * cell_list[None, :], count_xdim).astype(jnp.float32)
        / count_xdim
    )
    angles = 2.0 * math.pi * phases
    scaling = 1.0 / math.sqrt(count_xdim)
    return (
        (jnp.cos(angles) * scaling).astype(jnp.bfloat16),
        (jnp.sin(angles) * scaling).astype(jnp.bfloat16),
    )


def doubling_table():
    return jnp.where(jnp.arange(MODES, dtype=jnp.int32) > 0, 2.0, 1.0).astype(jnp.float32)


def gelu_slope(values):
    cumulative = 0.5 * (1.0 + lax.erf(values * 0.7071067811865476))
    bell_curve = jnp.exp(-0.5 * values * values) * 0.3989422804014327
    return cumulative + values * bell_curve


def forward_parts(field, cosines, sines):
    real_part = jnp.einsum("scxl,fx->slcf", field, cosines, preferred_element_type=jnp.float32)
    imag_part = -jnp.einsum("scxl,fx->slcf", field, sines, preferred_element_type=jnp.float32)
    return (real_part, imag_part)


def inverse_cells(values_real, values_imag, cosines, sines):
    first = jnp.einsum("slcf,fx->scxl", values_real, cosines, preferred_element_type=jnp.float32)
    second = jnp.einsum("slcf,fx->scxl", values_imag, sines, preferred_element_type=jnp.float32)
    return (first - second).astype(jnp.bfloat16)


def on_device(
    density, upstream, spectral_weight, moment_one, moment_two, skip_weight, skip_bias, mode_counts
):
    samples, channels, slab_rows, line_count = density.shape
    count_xdim = slab_rows * lax.axis_size("dom")
    cosines, sines = axis_parts(count_xdim)
    doubling = doubling_table()
    doubling_low = doubling.astype(jnp.bfloat16)
    counts_here = lax.dynamic_slice_in_dim(mode_counts, lax.axis_index("dp") * samples, samples, 0)
    keep_modes = (jnp.arange(MODES, dtype=jnp.int32)[None, :] < counts_here[:, None]).astype(
        jnp.float32
    )
    keep_wide = keep_modes[:, None, None, :]
    weight_short = spectral_weight.astype(jnp.bfloat16)
    group_low = collect(weight_short, "dom", 0)
    weight_low = lax.all_gather(group_low, "dp", axis=0, tiled=True)
    weight_low = weight_low.reshape(2, MODES, channels, channels)
    weight_real = weight_low[0]
    weight_imag = weight_low[1]
    density_lines, upstream_lines = in_one_piece((density, upstream), "dom", 3, 2, 0)
    real_part, imag_part = forward_parts(density_lines, cosines, sines)
    spec_real = real_part.astype(jnp.bfloat16)
    spec_imag = imag_part.astype(jnp.bfloat16)
    form = "slcf,fco->slof"
    mixed_real = jnp.einsum(
        form, spec_real, weight_real, preferred_element_type=jnp.float32
    ) - jnp.einsum(form, spec_imag, weight_imag, preferred_element_type=jnp.float32)
    mixed_imag = jnp.einsum(
        form, spec_imag, weight_real, preferred_element_type=jnp.float32
    ) + jnp.einsum(form, spec_real, weight_imag, preferred_element_type=jnp.float32)
    mixed_real = (mixed_real * keep_wide).astype(jnp.bfloat16) * doubling_low
    mixed_imag = (mixed_imag * keep_wide).astype(jnp.bfloat16) * doubling_low
    back_lines = inverse_cells(mixed_real, mixed_imag, cosines, sines)
    back_rows = lax.optimization_barrier(back_lines)
    skip_part = jnp.einsum(
        "oc,scxl->soxl", skip_weight, density_lines, preferred_element_type=jnp.float32
    )
    before = back_rows.astype(jnp.float32) + skip_part + skip_bias[None, :, None, None]
    gate_lines = (upstream_lines.astype(jnp.float32) * gelu_slope(before)).astype(jnp.bfloat16)
    grad_real, grad_imag = forward_parts(gate_lines, cosines, sines)
    scale = keep_wide * doubling
    grad_real = (grad_real * scale).astype(jnp.bfloat16)
    grad_imag = (grad_imag * scale).astype(jnp.bfloat16)
    outer = "slof,slcf->fco"
    part_real = jnp.einsum(
        outer, grad_real, spec_real, preferred_element_type=jnp.float32
    ) + jnp.einsum(outer, grad_imag, spec_imag, preferred_element_type=jnp.float32)
    part_imag = jnp.einsum(
        outer, grad_imag, spec_real, preferred_element_type=jnp.float32
    ) - jnp.einsum(outer, grad_real, spec_imag, preferred_element_type=jnp.float32)
    groups = lax.axis_size("dp")
    slabs = lax.axis_size("dom")
    rows_here = spectral_weight.shape[0]
    grad_local = jnp.stack([part_real, part_imag], 0).astype(jnp.bfloat16)
    grad_tiles = jnp.moveaxis(grad_local.reshape(groups, slabs, rows_here, channels), 1, 0)
    inner = "fco,slof->slcf"
    input_real = jnp.einsum(
        inner, weight_real, grad_real, preferred_element_type=jnp.float32
    ) + jnp.einsum(inner, weight_imag, grad_imag, preferred_element_type=jnp.float32)
    input_imag = jnp.einsum(
        inner, weight_real, grad_imag, preferred_element_type=jnp.float32
    ) - jnp.einsum(inner, weight_imag, grad_real, preferred_element_type=jnp.float32)
    input_lines = inverse_cells(
        input_real.astype(jnp.bfloat16), input_imag.astype(jnp.bfloat16), cosines, sines
    )
    input_rows = lax.optimization_barrier(input_lines)
    skip_back = jnp.einsum(
        "oc,soxl->scxl", skip_weight, gate_lines, preferred_element_type=jnp.float32
    )
    grad_lines = (input_rows.astype(jnp.float32) + skip_back).astype(jnp.bfloat16)
    group_grad = lax.all_to_all(grad_tiles, "dom", 0, 0, tiled=True)
    grad_lines, group_grad = lax.optimization_barrier((grad_lines, group_grad))
    input_grad = lax.all_to_all(grad_lines, "dom", split_axis=2, concat_axis=3, tiled=True)
    group_grad = group_grad.astype(jnp.float32).sum(axis=0)
    every_group = lax.all_gather(group_grad, "dp", axis=0, tiled=False)
    input_grad, every_group = lax.optimization_barrier((input_grad, every_group))
    mine = lax.dynamic_index_in_dim(every_group, lax.axis_index("dp"), 1, keepdims=False)
    weight_grad = mine.sum(axis=0)
    new_moment_one = beta_first * moment_one + (1.0 - beta_first) * weight_grad
    new_moment_two = beta_second * moment_two + (1.0 - beta_second) * weight_grad * weight_grad
    first_hat = new_moment_one / (1.0 - beta_first**STEP)
    second_hat = new_moment_two / (1.0 - beta_second**STEP)
    new_weight = spectral_weight - learn_rate * (
        first_hat / (jnp.sqrt(second_hat) + epsilon) + decay_rate * spectral_weight
    )
    return (input_grad, new_weight, new_moment_one, new_moment_two)


def solution(mesh):
    placed = (
        P("dp", None, "dom", None),
        P("dp", None, "dom", None),
        P(("dp", "dom"), None),
        P(("dp", "dom"), None),
        P(("dp", "dom"), None),
        P(),
        P(),
        P(),
    )
    return jax.shard_map(
        on_device,
        mesh=mesh,
        in_specs=placed,
        out_specs=(
            P("dp", None, "dom", None),
            P(("dp", "dom"), None),
            P(("dp", "dom"), None),
            P(("dp", "dom"), None),
        ),
        check_vma=False,
    )
```

```python
import math

import jax
import jax.numpy as jnp
from jax import lax
from jax.sharding import PartitionSpec as P

MODES = 16
STEP = 10


learn_rate = 0.01
beta_first = 0.9
beta_second = 0.95
decay_rate = 0.1
epsilon = 1e-08


def joined_along(tiles, dim):
    dims = list(tiles.shape[1:])
    dims[dim] *= tiles.shape[0]
    return jnp.moveaxis(tiles, 0, dim).reshape(dims)


def copy_for_each(shard, axis):
    copies = jnp.broadcast_to(shard, (lax.axis_size(axis), *shard.shape))
    return lax.all_to_all(copies, axis, split_axis=0, concat_axis=0, tiled=True)


def collect(shard, axis, dim):
    return joined_along(copy_for_each(shard, axis), dim)


def in_one_piece(arrays, axis, split_dim, concat_dim, along):
    both = jnp.concatenate(arrays, axis=along)
    result, at, done = (
        lax.all_to_all(both, axis, split_axis=split_dim, concat_axis=concat_dim, tiled=True),
        0,
        [],
    )
    for a in arrays:
        done.append(lax.slice_in_dim(result, at, at + a.shape[along], axis=along))
        at += a.shape[along]
    return tuple(done)


def split_up(shard, dim, length):
    dims = shard.shape
    tiles = shard.reshape(*dims[:dim], length, dims[dim] // length, *dims[dim + 1 :])
    return jnp.moveaxis(tiles, dim, 0)


def sum_at_owner(shard, axis, dim):
    tiles = split_up(shard, dim, lax.axis_size(axis))
    arrived = lax.all_to_all(tiles, axis, split_axis=0, concat_axis=0, tiled=True)
    return arrived.astype(jnp.float32).sum(axis=0)


def summed_on_arrival(shard, axis, dim):
    length = lax.axis_size(axis)
    tiles = lax.all_to_all(split_up(shard, dim, length), axis, 0, 0, tiled=True)
    return jnp.sum(tiles, axis=0)


def axis_parts(count_xdim):
    freq_list = jnp.arange(MODES, dtype=jnp.int32)
    cell_list = jnp.arange(count_xdim, dtype=jnp.int32)
    phases = (
        jnp.mod(freq_list[:, None] * cell_list[None, :], count_xdim).astype(jnp.float32)
        / count_xdim
    )
    angles = 2.0 * math.pi * phases
    scaling = 1.0 / math.sqrt(count_xdim)
    return (
        (jnp.cos(angles) * scaling).astype(jnp.bfloat16),
        (jnp.sin(angles) * scaling).astype(jnp.bfloat16),
    )


def doubling_table():
    return jnp.where(jnp.arange(MODES, dtype=jnp.int32) > 0, 2.0, 1.0).astype(jnp.float32)


def gelu_slope(values):
    cumulative = 0.5 * (1.0 + lax.erf(values * 0.7071067811865476))
    bell_curve = jnp.exp(-0.5 * values * values) * 0.3989422804014327
    return cumulative + values * bell_curve


def forward_parts(field, cosines, sines):
    real_part = jnp.einsum("scxl,fx->slcf", field, cosines, preferred_element_type=jnp.float32)
    imag_part = -jnp.einsum("scxl,fx->slcf", field, sines, preferred_element_type=jnp.float32)
    return (real_part, imag_part)


def inverse_cells(values_real, values_imag, cosines, sines):
    first = jnp.einsum("slcf,fx->scxl", values_real, cosines, preferred_element_type=jnp.float32)
    second = jnp.einsum("slcf,fx->scxl", values_imag, sines, preferred_element_type=jnp.float32)
    return (first - second).astype(jnp.bfloat16)


def on_device(
    density, upstream, spectral_weight, moment_one, moment_two, skip_weight, skip_bias, mode_counts
):
    samples, channels, slab_rows, line_count = density.shape
    count_xdim = slab_rows * lax.axis_size("dom")
    cosines, sines = axis_parts(count_xdim)
    doubling = doubling_table()
    doubling_low = doubling.astype(jnp.bfloat16)
    counts_here = lax.dynamic_slice_in_dim(mode_counts, lax.axis_index("dp") * samples, samples, 0)
    keep_modes = (jnp.arange(MODES, dtype=jnp.int32)[None, :] < counts_here[:, None]).astype(
        jnp.float32
    )
    weight_short = spectral_weight.astype(jnp.bfloat16)
    weight_short, keep_modes = lax.optimization_barrier((weight_short, keep_modes))
    keep_wide = keep_modes[:, None, None, :]
    group_low = collect(weight_short, "dom", 0)
    weight_low = lax.all_gather(group_low, "dp", axis=0, tiled=True)
    weight_low = weight_low.reshape(2, MODES, channels, channels)
    weight_real = weight_low[0]
    weight_imag = weight_low[1]
    density_lines, upstream_lines = in_one_piece((density, upstream), "dom", 3, 2, 0)
    real_part, imag_part = forward_parts(density_lines, cosines, sines)
    spec_real = real_part.astype(jnp.bfloat16)
    spec_imag = imag_part.astype(jnp.bfloat16)
    form = "slcf,fco->slof"
    mixed_real = jnp.einsum(
        form, spec_real, weight_real, preferred_element_type=jnp.float32
    ) - jnp.einsum(form, spec_imag, weight_imag, preferred_element_type=jnp.float32)
    mixed_imag = jnp.einsum(
        form, spec_imag, weight_real, preferred_element_type=jnp.float32
    ) + jnp.einsum(form, spec_real, weight_imag, preferred_element_type=jnp.float32)
    mixed_real = (mixed_real * keep_wide).astype(jnp.bfloat16) * doubling_low
    mixed_imag = (mixed_imag * keep_wide).astype(jnp.bfloat16) * doubling_low
    back_lines = inverse_cells(mixed_real, mixed_imag, cosines, sines)
    back_rows = lax.optimization_barrier(back_lines)
    skip_part = jnp.einsum(
        "oc,scxl->soxl", skip_weight, density_lines, preferred_element_type=jnp.float32
    )
    before = back_rows.astype(jnp.float32) + skip_part + skip_bias[None, :, None, None]
    gate_lines = (upstream_lines.astype(jnp.float32) * gelu_slope(before)).astype(jnp.bfloat16)
    grad_real, grad_imag = forward_parts(gate_lines, cosines, sines)
    scale = keep_wide * doubling
    grad_real = (grad_real * scale).astype(jnp.bfloat16)
    grad_imag = (grad_imag * scale).astype(jnp.bfloat16)
    outer = "slof,slcf->fco"
    part_real = jnp.einsum(
        outer, grad_real, spec_real, preferred_element_type=jnp.float32
    ) + jnp.einsum(outer, grad_imag, spec_imag, preferred_element_type=jnp.float32)
    part_imag = jnp.einsum(
        outer, grad_imag, spec_real, preferred_element_type=jnp.float32
    ) - jnp.einsum(outer, grad_real, spec_imag, preferred_element_type=jnp.float32)
    groups = lax.axis_size("dp")
    slabs = lax.axis_size("dom")
    rows_here = spectral_weight.shape[0]
    grad_local = jnp.stack([part_real, part_imag], 0).astype(jnp.bfloat16)
    grad_tiles = jnp.moveaxis(grad_local.reshape(groups, slabs, rows_here, channels), 1, 0)
    inner = "fco,slof->slcf"
    input_real = jnp.einsum(
        inner, weight_real, grad_real, preferred_element_type=jnp.float32
    ) + jnp.einsum(inner, weight_imag, grad_imag, preferred_element_type=jnp.float32)
    input_imag = jnp.einsum(
        inner, weight_real, grad_imag, preferred_element_type=jnp.float32
    ) - jnp.einsum(inner, weight_imag, grad_real, preferred_element_type=jnp.float32)
    input_lines = inverse_cells(
        input_real.astype(jnp.bfloat16), input_imag.astype(jnp.bfloat16), cosines, sines
    )
    input_rows = lax.optimization_barrier(input_lines)
    skip_back = jnp.einsum(
        "oc,soxl->scxl", skip_weight, gate_lines, preferred_element_type=jnp.float32
    )
    grad_lines = (input_rows.astype(jnp.float32) + skip_back).astype(jnp.bfloat16)
    group_grad = lax.all_to_all(grad_tiles, "dom", 0, 0, tiled=True)
    grad_lines, group_grad = lax.optimization_barrier((grad_lines, group_grad))
    input_grad = lax.all_to_all(grad_lines, "dom", split_axis=2, concat_axis=3, tiled=True)
    group_grad = group_grad.astype(jnp.float32).sum(axis=0)
    every_group = lax.all_gather(group_grad, "dp", axis=0, tiled=False)
    mine = lax.dynamic_index_in_dim(every_group, lax.axis_index("dp"), 1, keepdims=False)
    weight_grad = mine.sum(axis=0)
    new_moment_one = beta_first * moment_one + (1.0 - beta_first) * weight_grad
    new_moment_two = beta_second * moment_two + (1.0 - beta_second) * weight_grad * weight_grad
    first_hat = new_moment_one / (1.0 - beta_first**STEP)
    second_hat = new_moment_two / (1.0 - beta_second**STEP)
    new_weight = spectral_weight - learn_rate * (
        first_hat / (jnp.sqrt(second_hat) + epsilon) + decay_rate * spectral_weight
    )
    return lax.optimization_barrier((input_grad, new_weight, new_moment_one, new_moment_two))


def solution(mesh):
    placed = (
        P("dp", None, "dom", None),
        P("dp", None, "dom", None),
        P(("dp", "dom"), None),
        P(("dp", "dom"), None),
        P(("dp", "dom"), None),
        P(),
        P(),
        P(),
    )
    return jax.shard_map(
        on_device,
        mesh=mesh,
        in_specs=placed,
        out_specs=(
            P("dp", None, "dom", None),
            P(("dp", "dom"), None),
            P(("dp", "dom"), None),
            P(("dp", "dom"), None),
        ),
        check_vma=False,
    )
```

```python
import math

import jax
import jax.numpy as jnp
from jax import lax
from jax.sharding import PartitionSpec as P

MODES = 16
STEP = 10


learn_rate = 0.01
beta_first = 0.9
beta_second = 0.95
decay_rate = 0.1
epsilon = 1e-08


def joined_along(tiles, dim):
    dims = list(tiles.shape[1:])
    dims[dim] *= tiles.shape[0]
    return jnp.moveaxis(tiles, 0, dim).reshape(dims)


def copy_for_each(shard, axis):
    copies = jnp.broadcast_to(shard, (lax.axis_size(axis), *shard.shape))
    return lax.all_to_all(copies, axis, split_axis=0, concat_axis=0, tiled=True)


def collect(shard, axis, dim):
    return joined_along(copy_for_each(shard, axis), dim)


def in_one_piece(arrays, axis, split_dim, concat_dim, along):
    both = jnp.concatenate(arrays, axis=along)
    result, at, done = (
        lax.all_to_all(both, axis, split_axis=split_dim, concat_axis=concat_dim, tiled=True),
        0,
        [],
    )
    for a in arrays:
        done.append(lax.slice_in_dim(result, at, at + a.shape[along], axis=along))
        at += a.shape[along]
    return tuple(done)


def split_up(shard, dim, length):
    dims = shard.shape
    tiles = shard.reshape(*dims[:dim], length, dims[dim] // length, *dims[dim + 1 :])
    return jnp.moveaxis(tiles, dim, 0)


def sum_at_owner(shard, axis, dim):
    tiles = split_up(shard, dim, lax.axis_size(axis))
    arrived = lax.all_to_all(tiles, axis, split_axis=0, concat_axis=0, tiled=True)
    return arrived.astype(jnp.float32).sum(axis=0)


def summed_on_arrival(shard, axis, dim):
    length = lax.axis_size(axis)
    tiles = lax.all_to_all(split_up(shard, dim, length), axis, 0, 0, tiled=True)
    return jnp.sum(tiles, axis=0)


def axis_parts(count_xdim):
    freq_list = jnp.arange(MODES, dtype=jnp.int32)
    cell_list = jnp.arange(count_xdim, dtype=jnp.int32)
    phases = (
        jnp.mod(freq_list[:, None] * cell_list[None, :], count_xdim).astype(jnp.float32)
        / count_xdim
    )
    angles = 2.0 * math.pi * phases
    scaling = 1.0 / math.sqrt(count_xdim)
    return (
        (jnp.cos(angles) * scaling).astype(jnp.bfloat16),
        (jnp.sin(angles) * scaling).astype(jnp.bfloat16),
    )


def doubling_table():
    return jnp.where(jnp.arange(MODES, dtype=jnp.int32) > 0, 2.0, 1.0).astype(jnp.float32)


def gelu_slope(values):
    cumulative = 0.5 * (1.0 + lax.erf(values * 0.7071067811865476))
    bell_curve = jnp.exp(-0.5 * values * values) * 0.3989422804014327
    return cumulative + values * bell_curve


def forward_parts(field, cosines, sines):
    real_part = jnp.einsum("scxl,fx->slcf", field, cosines, preferred_element_type=jnp.float32)
    imag_part = -jnp.einsum("scxl,fx->slcf", field, sines, preferred_element_type=jnp.float32)
    return (real_part, imag_part)


def inverse_cells(values_real, values_imag, cosines, sines):
    first = jnp.einsum("slcf,fx->scxl", values_real, cosines, preferred_element_type=jnp.float32)
    second = jnp.einsum("slcf,fx->scxl", values_imag, sines, preferred_element_type=jnp.float32)
    return (first - second).astype(jnp.bfloat16)


def on_device(
    density, upstream, spectral_weight, moment_one, moment_two, skip_weight, skip_bias, mode_counts
):
    samples, channels, slab_rows, line_count = density.shape
    count_xdim = slab_rows * lax.axis_size("dom")
    cosines, sines = axis_parts(count_xdim)
    doubling = doubling_table()
    doubling_low = doubling.astype(jnp.bfloat16)
    counts_here = lax.dynamic_slice_in_dim(mode_counts, lax.axis_index("dp") * samples, samples, 0)
    keep_modes = (jnp.arange(MODES, dtype=jnp.int32)[None, :] < counts_here[:, None]).astype(
        jnp.float32
    )
    keep_wide = keep_modes[:, None, None, :]
    weight_short = spectral_weight.astype(jnp.bfloat16)
    group_low = collect(weight_short, "dom", 0)
    weight_low = lax.all_gather(group_low, "dp", axis=0, tiled=True)
    weight_low = weight_low.reshape(2, MODES, channels, channels)
    weight_real = weight_low[0]
    weight_imag = weight_low[1]
    density_lines, upstream_lines = in_one_piece((density, upstream), "dom", 3, 2, 0)
    real_part, imag_part = forward_parts(density_lines, cosines, sines)
    spec_real = real_part.astype(jnp.bfloat16)
    spec_imag = imag_part.astype(jnp.bfloat16)
    form = "slcf,fco->slof"
    mixed_real = jnp.einsum(
        form, spec_real, weight_real, preferred_element_type=jnp.float32
    ) - jnp.einsum(form, spec_imag, weight_imag, preferred_element_type=jnp.float32)
    mixed_imag = jnp.einsum(
        form, spec_imag, weight_real, preferred_element_type=jnp.float32
    ) + jnp.einsum(form, spec_real, weight_imag, preferred_element_type=jnp.float32)
    mixed_real = (mixed_real * keep_wide).astype(jnp.bfloat16) * doubling_low
    mixed_imag = (mixed_imag * keep_wide).astype(jnp.bfloat16) * doubling_low
    back_lines = inverse_cells(mixed_real, mixed_imag, cosines, sines)
    back_rows = lax.optimization_barrier(back_lines)
    skip_part = jnp.einsum(
        "oc,scxl->soxl", skip_weight, density_lines, preferred_element_type=jnp.float32
    )
    before = back_rows.astype(jnp.float32) + skip_part + skip_bias[None, :, None, None]
    gate_lines = (upstream_lines.astype(jnp.float32) * gelu_slope(before)).astype(jnp.bfloat16)
    grad_real, grad_imag = forward_parts(gate_lines, cosines, sines)
    scale = keep_wide * doubling
    grad_real = (grad_real * scale).astype(jnp.bfloat16)
    grad_imag = (grad_imag * scale).astype(jnp.bfloat16)
    inner = "fco,slof->slcf"
    input_real = jnp.einsum(
        inner, weight_real, grad_real, preferred_element_type=jnp.float32
    ) + jnp.einsum(inner, weight_imag, grad_imag, preferred_element_type=jnp.float32)
    input_imag = jnp.einsum(
        inner, weight_real, grad_imag, preferred_element_type=jnp.float32
    ) - jnp.einsum(inner, weight_imag, grad_real, preferred_element_type=jnp.float32)
    input_lines = inverse_cells(
        input_real.astype(jnp.bfloat16), input_imag.astype(jnp.bfloat16), cosines, sines
    )
    input_rows = lax.optimization_barrier(input_lines)
    skip_back = jnp.einsum(
        "oc,soxl->scxl", skip_weight, gate_lines, preferred_element_type=jnp.float32
    )
    grad_lines = (input_rows.astype(jnp.float32) + skip_back).astype(jnp.bfloat16)
    groups = lax.axis_size("dp")
    slabs = lax.axis_size("dom")
    rows_here = spectral_weight.shape[0]
    input_grad = lax.all_to_all(grad_lines, "dom", split_axis=2, concat_axis=3, tiled=True)
    packed = jnp.stack([grad_real, grad_imag, spec_real, spec_imag], 0)
    every_group = lax.all_gather(packed, "dp", axis=1, tiled=True)
    input_grad, every_group = lax.optimization_barrier((input_grad, every_group))
    group_real, group_imag, group_spec_real, group_spec_imag = (every_group[i] for i in range(4))
    outer = "slof,slcf->fco"
    part_real = jnp.einsum(
        outer, group_real, group_spec_real, preferred_element_type=jnp.float32
    ) + jnp.einsum(outer, group_imag, group_spec_imag, preferred_element_type=jnp.float32)
    part_imag = jnp.einsum(
        outer, group_imag, group_spec_real, preferred_element_type=jnp.float32
    ) - jnp.einsum(outer, group_real, group_spec_imag, preferred_element_type=jnp.float32)
    group_rows = jnp.stack([part_real, part_imag], 0).reshape(groups, slabs, rows_here, channels)
    own_rows = lax.dynamic_index_in_dim(group_rows, lax.axis_index("dp"), 0, keepdims=False)
    weight_grad = lax.all_to_all(own_rows, "dom", 0, 0, tiled=True).reshape(
        slabs, rows_here, channels
    ).sum(axis=0)
    new_moment_one = beta_first * moment_one + (1.0 - beta_first) * weight_grad
    new_moment_two = beta_second * moment_two + (1.0 - beta_second) * weight_grad * weight_grad
    first_hat = new_moment_one / (1.0 - beta_first**STEP)
    second_hat = new_moment_two / (1.0 - beta_second**STEP)
    new_weight = spectral_weight - learn_rate * (
        first_hat / (jnp.sqrt(second_hat) + epsilon) + decay_rate * spectral_weight
    )
    return (input_grad, new_weight, new_moment_one, new_moment_two)


def solution(mesh):
    placed = (
        P("dp", None, "dom", None),
        P("dp", None, "dom", None),
        P(("dp", "dom"), None),
        P(("dp", "dom"), None),
        P(("dp", "dom"), None),
        P(),
        P(),
        P(),
    )
    return jax.shard_map(
        on_device,
        mesh=mesh,
        in_specs=placed,
        out_specs=(
            P("dp", None, "dom", None),
            P(("dp", "dom"), None),
            P(("dp", "dom"), None),
            P(("dp", "dom"), None),
        ),
        check_vma=False,
    )
```

```python
import math

import jax
import jax.numpy as jnp
from jax import lax
from jax.sharding import PartitionSpec as P

MODES = 16
STEP = 10


learn_rate = 0.01
beta_first = 0.9
beta_second = 0.95
decay_rate = 0.1
epsilon = 1e-08


def joined_along(tiles, dim):
    dims = list(tiles.shape[1:])
    dims[dim] *= tiles.shape[0]
    return jnp.moveaxis(tiles, 0, dim).reshape(dims)


def copy_for_each(shard, axis):
    copies = jnp.broadcast_to(shard, (lax.axis_size(axis), *shard.shape))
    return lax.all_to_all(copies, axis, split_axis=0, concat_axis=0, tiled=True)


def collect(shard, axis, dim):
    return joined_along(copy_for_each(shard, axis), dim)


def in_one_piece(arrays, axis, split_dim, concat_dim, along):
    both = jnp.concatenate(arrays, axis=along)
    result, at, done = (
        lax.all_to_all(both, axis, split_axis=split_dim, concat_axis=concat_dim, tiled=True),
        0,
        [],
    )
    for a in arrays:
        done.append(lax.slice_in_dim(result, at, at + a.shape[along], axis=along))
        at += a.shape[along]
    return tuple(done)


def split_up(shard, dim, length):
    dims = shard.shape
    tiles = shard.reshape(*dims[:dim], length, dims[dim] // length, *dims[dim + 1 :])
    return jnp.moveaxis(tiles, dim, 0)


def sum_at_owner(shard, axis, dim):
    tiles = split_up(shard, dim, lax.axis_size(axis))
    arrived = lax.all_to_all(tiles, axis, split_axis=0, concat_axis=0, tiled=True)
    return arrived.astype(jnp.float32).sum(axis=0)


def summed_on_arrival(shard, axis, dim):
    length = lax.axis_size(axis)
    tiles = lax.all_to_all(split_up(shard, dim, length), axis, 0, 0, tiled=True)
    return jnp.sum(tiles, axis=0)


def axis_parts(count_xdim):
    freq_list = jnp.arange(MODES, dtype=jnp.int32)
    cell_list = jnp.arange(count_xdim, dtype=jnp.int32)
    phases = (
        jnp.mod(freq_list[:, None] * cell_list[None, :], count_xdim).astype(jnp.float32)
        / count_xdim
    )
    angles = 2.0 * math.pi * phases
    scaling = 1.0 / math.sqrt(count_xdim)
    return (
        (jnp.cos(angles) * scaling).astype(jnp.bfloat16),
        (jnp.sin(angles) * scaling).astype(jnp.bfloat16),
    )


def doubling_table():
    return jnp.where(jnp.arange(MODES, dtype=jnp.int32) > 0, 2.0, 1.0).astype(jnp.float32)


def gelu_slope(values):
    cumulative = 0.5 * (1.0 + lax.erf(values * 0.7071067811865476))
    bell_curve = jnp.exp(-0.5 * values * values) * 0.3989422804014327
    return cumulative + values * bell_curve


def forward_parts(field, cosines, sines):
    basis = jnp.concatenate([cosines, -sines], axis=0)
    both = jnp.einsum("scxl,gx->slcg", field, basis, preferred_element_type=jnp.float32)
    return (both[..., :MODES], both[..., MODES:])


def inverse_cells(values_real, values_imag, cosines, sines):
    basis = jnp.concatenate([cosines, -sines], axis=0)
    both = jnp.concatenate([values_real, values_imag], axis=3)
    return jnp.einsum("slcg,gx->scxl", both, basis, preferred_element_type=jnp.float32).astype(
        jnp.bfloat16
    )


def on_device(
    density, upstream, spectral_weight, moment_one, moment_two, skip_weight, skip_bias, mode_counts
):
    samples, channels, slab_rows, line_count = density.shape
    count_xdim = slab_rows * lax.axis_size("dom")
    cosines, sines = axis_parts(count_xdim)
    doubling = doubling_table()
    doubling_low = doubling.astype(jnp.bfloat16)
    counts_here = lax.dynamic_slice_in_dim(mode_counts, lax.axis_index("dp") * samples, samples, 0)
    keep_modes = (jnp.arange(MODES, dtype=jnp.int32)[None, :] < counts_here[:, None]).astype(
        jnp.float32
    )
    keep_wide = keep_modes[:, None, None, :]
    weight_short = spectral_weight.astype(jnp.bfloat16)
    group_low = collect(weight_short, "dom", 0)
    weight_low = lax.all_gather(group_low, "dp", axis=0, tiled=True)
    weight_low = weight_low.reshape(2, MODES, channels, channels)
    weight_real = weight_low[0]
    weight_imag = weight_low[1]
    density_lines, upstream_lines = in_one_piece((density, upstream), "dom", 3, 2, 0)
    real_part, imag_part = forward_parts(density_lines, cosines, sines)
    spec_real = real_part.astype(jnp.bfloat16)
    spec_imag = imag_part.astype(jnp.bfloat16)
    form = "slcf,fco->slof"
    mixed_real = jnp.einsum(
        form, spec_real, weight_real, preferred_element_type=jnp.float32
    ) - jnp.einsum(form, spec_imag, weight_imag, preferred_element_type=jnp.float32)
    mixed_imag = jnp.einsum(
        form, spec_imag, weight_real, preferred_element_type=jnp.float32
    ) + jnp.einsum(form, spec_real, weight_imag, preferred_element_type=jnp.float32)
    mixed_real = (mixed_real * keep_wide).astype(jnp.bfloat16) * doubling_low
    mixed_imag = (mixed_imag * keep_wide).astype(jnp.bfloat16) * doubling_low
    back_lines = inverse_cells(mixed_real, mixed_imag, cosines, sines)
    back_rows = lax.optimization_barrier(back_lines)
    skip_part = jnp.einsum(
        "oc,scxl->soxl", skip_weight, density_lines, preferred_element_type=jnp.float32
    )
    before = back_rows.astype(jnp.float32) + skip_part + skip_bias[None, :, None, None]
    gate_lines = (upstream_lines.astype(jnp.float32) * gelu_slope(before)).astype(jnp.bfloat16)
    grad_real, grad_imag = forward_parts(gate_lines, cosines, sines)
    scale = keep_wide * doubling
    grad_real = (grad_real * scale).astype(jnp.bfloat16)
    grad_imag = (grad_imag * scale).astype(jnp.bfloat16)
    outer = "slof,slcf->fco"
    part_real = jnp.einsum(
        outer, grad_real, spec_real, preferred_element_type=jnp.float32
    ) + jnp.einsum(outer, grad_imag, spec_imag, preferred_element_type=jnp.float32)
    part_imag = jnp.einsum(
        outer, grad_imag, spec_real, preferred_element_type=jnp.float32
    ) - jnp.einsum(outer, grad_real, spec_imag, preferred_element_type=jnp.float32)
    groups = lax.axis_size("dp")
    slabs = lax.axis_size("dom")
    rows_here = spectral_weight.shape[0]
    grad_local = jnp.stack([part_real, part_imag], 0).astype(jnp.bfloat16)
    grad_tiles = jnp.moveaxis(grad_local.reshape(groups, slabs, rows_here, channels), 1, 0)
    inner = "fco,slof->slcf"
    input_real = jnp.einsum(
        inner, weight_real, grad_real, preferred_element_type=jnp.float32
    ) + jnp.einsum(inner, weight_imag, grad_imag, preferred_element_type=jnp.float32)
    input_imag = jnp.einsum(
        inner, weight_real, grad_imag, preferred_element_type=jnp.float32
    ) - jnp.einsum(inner, weight_imag, grad_real, preferred_element_type=jnp.float32)
    input_lines = inverse_cells(
        input_real.astype(jnp.bfloat16), input_imag.astype(jnp.bfloat16), cosines, sines
    )
    input_rows = lax.optimization_barrier(input_lines)
    skip_back = jnp.einsum(
        "oc,soxl->scxl", skip_weight, gate_lines, preferred_element_type=jnp.float32
    )
    grad_lines = (input_rows.astype(jnp.float32) + skip_back).astype(jnp.bfloat16)
    group_grad = lax.all_to_all(grad_tiles, "dom", 0, 0, tiled=True)
    grad_lines, group_grad = lax.optimization_barrier((grad_lines, group_grad))
    input_grad = lax.all_to_all(grad_lines, "dom", split_axis=2, concat_axis=3, tiled=True)
    group_grad = group_grad.astype(jnp.float32).sum(axis=0)
    every_group = lax.all_gather(group_grad, "dp", axis=0, tiled=False)
    mine = lax.dynamic_index_in_dim(every_group, lax.axis_index("dp"), 1, keepdims=False)
    weight_grad = mine.sum(axis=0)
    new_moment_one = beta_first * moment_one + (1.0 - beta_first) * weight_grad
    new_moment_two = beta_second * moment_two + (1.0 - beta_second) * weight_grad * weight_grad
    first_hat = new_moment_one / (1.0 - beta_first**STEP)
    second_hat = new_moment_two / (1.0 - beta_second**STEP)
    new_weight = spectral_weight - learn_rate * (
        first_hat / (jnp.sqrt(second_hat) + epsilon) + decay_rate * spectral_weight
    )
    return lax.optimization_barrier((input_grad, new_weight, new_moment_one, new_moment_two))


def solution(mesh):
    placed = (
        P("dp", None, "dom", None),
        P("dp", None, "dom", None),
        P(("dp", "dom"), None),
        P(("dp", "dom"), None),
        P(("dp", "dom"), None),
        P(),
        P(),
        P(),
    )
    return jax.shard_map(
        on_device,
        mesh=mesh,
        in_specs=placed,
        out_specs=(
            P("dp", None, "dom", None),
            P(("dp", "dom"), None),
            P(("dp", "dom"), None),
            P(("dp", "dom"), None),
        ),
        check_vma=False,
    )
```

```python
import math

import jax
import jax.numpy as jnp
from jax import lax
from jax.sharding import PartitionSpec as P

MODES = 16
STEP = 10


learn_rate = 0.01
beta_first = 0.9
beta_second = 0.95
decay_rate = 0.1
epsilon = 1e-08


def joined_along(tiles, dim):
    dims = list(tiles.shape[1:])
    dims[dim] *= tiles.shape[0]
    return jnp.moveaxis(tiles, 0, dim).reshape(dims)


def copy_for_each(shard, axis):
    copies = jnp.broadcast_to(shard, (lax.axis_size(axis), *shard.shape))
    return lax.all_to_all(copies, axis, split_axis=0, concat_axis=0, tiled=True)


def collect(shard, axis, dim):
    return joined_along(copy_for_each(shard, axis), dim)


def in_one_piece(arrays, axis, split_dim, concat_dim, along):
    both = jnp.concatenate(arrays, axis=along)
    result, at, done = (
        lax.all_to_all(both, axis, split_axis=split_dim, concat_axis=concat_dim, tiled=True),
        0,
        [],
    )
    for a in arrays:
        done.append(lax.slice_in_dim(result, at, at + a.shape[along], axis=along))
        at += a.shape[along]
    return tuple(done)


def split_up(shard, dim, length):
    dims = shard.shape
    tiles = shard.reshape(*dims[:dim], length, dims[dim] // length, *dims[dim + 1 :])
    return jnp.moveaxis(tiles, dim, 0)


def sum_at_owner(shard, axis, dim):
    tiles = split_up(shard, dim, lax.axis_size(axis))
    arrived = lax.all_to_all(tiles, axis, split_axis=0, concat_axis=0, tiled=True)
    return arrived.astype(jnp.float32).sum(axis=0)


def summed_on_arrival(shard, axis, dim):
    length = lax.axis_size(axis)
    tiles = lax.all_to_all(split_up(shard, dim, length), axis, 0, 0, tiled=True)
    return jnp.sum(tiles, axis=0)


def axis_parts(count_xdim):
    freq_list = jnp.arange(MODES, dtype=jnp.int32)
    cell_list = jnp.arange(count_xdim, dtype=jnp.int32)
    phases = (
        jnp.mod(freq_list[:, None] * cell_list[None, :], count_xdim).astype(jnp.float32)
        / count_xdim
    )
    angles = 2.0 * math.pi * phases
    scaling = 1.0 / math.sqrt(count_xdim)
    return (
        (jnp.cos(angles) * scaling).astype(jnp.bfloat16),
        (jnp.sin(angles) * scaling).astype(jnp.bfloat16),
    )


def doubling_table():
    return jnp.where(jnp.arange(MODES, dtype=jnp.int32) > 0, 2.0, 1.0).astype(jnp.float32)


def gelu_slope(values):
    cumulative = 0.5 * (1.0 + lax.erf(values * 0.7071067811865476))
    bell_curve = jnp.exp(-0.5 * values * values) * 0.3989422804014327
    return cumulative + values * bell_curve


def forward_parts(field, cosines, sines):
    basis = jnp.concatenate([cosines, -sines], axis=0)
    both = jnp.einsum("scxl,gx->slcg", field, basis, preferred_element_type=jnp.float32)
    return (both[..., :MODES], both[..., MODES:])


def inverse_cells(values_real, values_imag, cosines, sines):
    basis = jnp.concatenate([cosines, -sines], axis=0)
    both = jnp.concatenate([values_real, values_imag], axis=3)
    return jnp.einsum("slcg,gx->scxl", both, basis, preferred_element_type=jnp.float32).astype(
        jnp.bfloat16
    )


def on_device(
    density, upstream, spectral_weight, moment_one, moment_two, skip_weight, skip_bias, mode_counts
):
    samples, channels, slab_rows, line_count = density.shape
    count_xdim = slab_rows * lax.axis_size("dom")
    cosines, sines = axis_parts(count_xdim)
    doubling = doubling_table()
    doubling_low = doubling.astype(jnp.bfloat16)
    counts_here = lax.dynamic_slice_in_dim(mode_counts, lax.axis_index("dp") * samples, samples, 0)
    keep_modes = (jnp.arange(MODES, dtype=jnp.int32)[None, :] < counts_here[:, None]).astype(
        jnp.float32
    )
    keep_wide = keep_modes[:, None, None, :]
    weight_short = spectral_weight.astype(jnp.bfloat16)
    density_lines, upstream_lines = in_one_piece((density, upstream), "dom", 3, 2, 0)
    column_low = lax.all_gather(weight_short, "dp", axis=0, tiled=False)
    column_low, density_lines, upstream_lines = lax.optimization_barrier(
        (column_low, density_lines, upstream_lines)
    )
    every_low = copy_for_each(column_low, "dom")
    weight_low = jnp.moveaxis(every_low, 0, 1).reshape(2, MODES, channels, channels)
    weight_real = weight_low[0]
    weight_imag = weight_low[1]
    real_part, imag_part = forward_parts(density_lines, cosines, sines)
    spec_real = real_part.astype(jnp.bfloat16)
    spec_imag = imag_part.astype(jnp.bfloat16)
    form = "slcf,fco->slof"
    mixed_real = jnp.einsum(
        form, spec_real, weight_real, preferred_element_type=jnp.float32
    ) - jnp.einsum(form, spec_imag, weight_imag, preferred_element_type=jnp.float32)
    mixed_imag = jnp.einsum(
        form, spec_imag, weight_real, preferred_element_type=jnp.float32
    ) + jnp.einsum(form, spec_real, weight_imag, preferred_element_type=jnp.float32)
    mixed_real = (mixed_real * keep_wide).astype(jnp.bfloat16) * doubling_low
    mixed_imag = (mixed_imag * keep_wide).astype(jnp.bfloat16) * doubling_low
    back_lines = inverse_cells(mixed_real, mixed_imag, cosines, sines)
    back_rows = lax.optimization_barrier(back_lines)
    skip_part = jnp.einsum(
        "oc,scxl->soxl", skip_weight, density_lines, preferred_element_type=jnp.float32
    )
    before = back_rows.astype(jnp.float32) + skip_part + skip_bias[None, :, None, None]
    gate_lines = (upstream_lines.astype(jnp.float32) * gelu_slope(before)).astype(jnp.bfloat16)
    grad_real, grad_imag = forward_parts(gate_lines, cosines, sines)
    scale = keep_wide * doubling
    grad_real = (grad_real * scale).astype(jnp.bfloat16)
    grad_imag = (grad_imag * scale).astype(jnp.bfloat16)
    outer = "slof,slcf->fco"
    part_real = jnp.einsum(
        outer, grad_real, spec_real, preferred_element_type=jnp.float32
    ) + jnp.einsum(outer, grad_imag, spec_imag, preferred_element_type=jnp.float32)
    part_imag = jnp.einsum(
        outer, grad_imag, spec_real, preferred_element_type=jnp.float32
    ) - jnp.einsum(outer, grad_real, spec_imag, preferred_element_type=jnp.float32)
    groups = lax.axis_size("dp")
    slabs = lax.axis_size("dom")
    rows_here = spectral_weight.shape[0]
    grad_local = jnp.stack([part_real, part_imag], 0).astype(jnp.bfloat16)
    grad_tiles = jnp.moveaxis(grad_local.reshape(groups, slabs, rows_here, channels), 1, 0)
    inner = "fco,slof->slcf"
    input_real = jnp.einsum(
        inner, weight_real, grad_real, preferred_element_type=jnp.float32
    ) + jnp.einsum(inner, weight_imag, grad_imag, preferred_element_type=jnp.float32)
    input_imag = jnp.einsum(
        inner, weight_real, grad_imag, preferred_element_type=jnp.float32
    ) - jnp.einsum(inner, weight_imag, grad_real, preferred_element_type=jnp.float32)
    input_lines = inverse_cells(
        input_real.astype(jnp.bfloat16), input_imag.astype(jnp.bfloat16), cosines, sines
    )
    input_rows = lax.optimization_barrier(input_lines)
    skip_back = jnp.einsum(
        "oc,soxl->scxl", skip_weight, gate_lines, preferred_element_type=jnp.float32
    )
    grad_lines = (input_rows.astype(jnp.float32) + skip_back).astype(jnp.bfloat16)
    group_grad = lax.all_to_all(grad_tiles, "dom", 0, 0, tiled=True)
    grad_lines, group_grad = lax.optimization_barrier((grad_lines, group_grad))
    input_grad = lax.all_to_all(grad_lines, "dom", split_axis=2, concat_axis=3, tiled=True)
    group_grad = group_grad.astype(jnp.float32).sum(axis=0)
    every_group = lax.all_gather(group_grad, "dp", axis=0, tiled=False)
    mine = lax.dynamic_index_in_dim(every_group, lax.axis_index("dp"), 1, keepdims=False)
    weight_grad = mine.sum(axis=0)
    new_moment_one = beta_first * moment_one + (1.0 - beta_first) * weight_grad
    new_moment_two = beta_second * moment_two + (1.0 - beta_second) * weight_grad * weight_grad
    first_hat = new_moment_one / (1.0 - beta_first**STEP)
    second_hat = new_moment_two / (1.0 - beta_second**STEP)
    new_weight = spectral_weight - learn_rate * (
        first_hat / (jnp.sqrt(second_hat) + epsilon) + decay_rate * spectral_weight
    )
    return lax.optimization_barrier((input_grad, new_weight, new_moment_one, new_moment_two))


def solution(mesh):
    placed = (
        P("dp", None, "dom", None),
        P("dp", None, "dom", None),
        P(("dp", "dom"), None),
        P(("dp", "dom"), None),
        P(("dp", "dom"), None),
        P(),
        P(),
        P(),
    )
    return jax.shard_map(
        on_device,
        mesh=mesh,
        in_specs=placed,
        out_specs=(
            P("dp", None, "dom", None),
            P(("dp", "dom"), None),
            P(("dp", "dom"), None),
            P(("dp", "dom"), None),
        ),
        check_vma=False,
    )
```

```python
import math

import jax
import jax.numpy as jnp
from jax import lax
from jax.sharding import PartitionSpec as P

MODES = 16
STEP = 10


learn_rate = 0.01
beta_first = 0.9
beta_second = 0.95
decay_rate = 0.1
epsilon = 1e-08


def joined_along(tiles, dim):
    dims = list(tiles.shape[1:])
    dims[dim] *= tiles.shape[0]
    return jnp.moveaxis(tiles, 0, dim).reshape(dims)


def copy_for_each(shard, axis):
    copies = jnp.broadcast_to(shard, (lax.axis_size(axis), *shard.shape))
    return lax.all_to_all(copies, axis, split_axis=0, concat_axis=0, tiled=True)


def collect(shard, axis, dim):
    return joined_along(copy_for_each(shard, axis), dim)


def in_one_piece(arrays, axis, split_dim, concat_dim, along):
    both = jnp.concatenate(arrays, axis=along)
    result, at, done = (
        lax.all_to_all(both, axis, split_axis=split_dim, concat_axis=concat_dim, tiled=True),
        0,
        [],
    )
    for a in arrays:
        done.append(lax.slice_in_dim(result, at, at + a.shape[along], axis=along))
        at += a.shape[along]
    return tuple(done)


def split_up(shard, dim, length):
    dims = shard.shape
    tiles = shard.reshape(*dims[:dim], length, dims[dim] // length, *dims[dim + 1 :])
    return jnp.moveaxis(tiles, dim, 0)


def sum_at_owner(shard, axis, dim):
    tiles = split_up(shard, dim, lax.axis_size(axis))
    arrived = lax.all_to_all(tiles, axis, split_axis=0, concat_axis=0, tiled=True)
    return arrived.astype(jnp.float32).sum(axis=0)


def summed_on_arrival(shard, axis, dim):
    length = lax.axis_size(axis)
    tiles = lax.all_to_all(split_up(shard, dim, length), axis, 0, 0, tiled=True)
    return jnp.sum(tiles, axis=0)


def axis_parts(count_xdim):
    freq_list = jnp.arange(MODES, dtype=jnp.int32)
    cell_list = jnp.arange(count_xdim, dtype=jnp.int32)
    phases = (
        jnp.mod(freq_list[:, None] * cell_list[None, :], count_xdim).astype(jnp.float32)
        / count_xdim
    )
    angles = 2.0 * math.pi * phases
    scaling = 1.0 / math.sqrt(count_xdim)
    return (
        (jnp.cos(angles) * scaling).astype(jnp.bfloat16),
        (jnp.sin(angles) * scaling).astype(jnp.bfloat16),
    )


def doubling_table():
    return jnp.where(jnp.arange(MODES, dtype=jnp.int32) > 0, 2.0, 1.0).astype(jnp.float32)


def gelu_slope(values):
    cumulative = 0.5 * (1.0 + lax.erf(values * 0.7071067811865476))
    bell_curve = jnp.exp(-0.5 * values * values) * 0.3989422804014327
    return cumulative + values * bell_curve


def forward_parts(field, cosines, sines):
    basis = jnp.concatenate([cosines, -sines], axis=0)
    both = jnp.einsum("scxl,gx->slcg", field, basis, preferred_element_type=jnp.float32)
    return (both[..., :MODES], both[..., MODES:])


def inverse_cells(values_real, values_imag, cosines, sines):
    basis = jnp.concatenate([cosines, -sines], axis=0)
    both = jnp.concatenate([values_real, values_imag], axis=3)
    return jnp.einsum("slcg,gx->scxl", both, basis, preferred_element_type=jnp.float32).astype(
        jnp.bfloat16
    )


def on_device(
    density, upstream, spectral_weight, moment_one, moment_two, skip_weight, skip_bias, mode_counts
):
    samples, channels, slab_rows, line_count = density.shape
    count_xdim = slab_rows * lax.axis_size("dom")
    cosines, sines = axis_parts(count_xdim)
    doubling = doubling_table()
    doubling_low = doubling.astype(jnp.bfloat16)
    counts_here = lax.dynamic_slice_in_dim(mode_counts, lax.axis_index("dp") * samples, samples, 0)
    keep_modes = (jnp.arange(MODES, dtype=jnp.int32)[None, :] < counts_here[:, None]).astype(
        jnp.float32
    )
    keep_wide = keep_modes[:, None, None, :]
    weight_short = spectral_weight.astype(jnp.bfloat16)
    rows_here = spectral_weight.shape[0]
    column_low = lax.all_gather(weight_short, "dp", axis=0, tiled=False)
    tile_shape = (channels, slab_rows, line_count // lax.axis_size("dom"))
    column_tiles = jnp.broadcast_to(
        column_low.reshape(channels, slab_rows, 1, tile_shape[2]),
        (channels, slab_rows, lax.axis_size("dom"), tile_shape[2]),
    ).reshape(density.shape)
    density_lines, upstream_lines, column_lines = in_one_piece(
        (density, upstream, column_tiles), "dom", 3, 2, 0
    )
    every_low = column_lines.reshape(channels, lax.axis_size("dom"), *tile_shape[1:])
    every_low = jnp.moveaxis(every_low, 1, 0).reshape(lax.axis_size("dom"), -1, rows_here, channels)
    weight_low = jnp.moveaxis(every_low, 0, 1).reshape(2, MODES, channels, channels)
    weight_real = weight_low[0]
    weight_imag = weight_low[1]
    real_part, imag_part = forward_parts(density_lines, cosines, sines)
    spec_real = real_part.astype(jnp.bfloat16)
    spec_imag = imag_part.astype(jnp.bfloat16)
    form = "slcf,fco->slof"
    mixed_real = jnp.einsum(
        form, spec_real, weight_real, preferred_element_type=jnp.float32
    ) - jnp.einsum(form, spec_imag, weight_imag, preferred_element_type=jnp.float32)
    mixed_imag = jnp.einsum(
        form, spec_imag, weight_real, preferred_element_type=jnp.float32
    ) + jnp.einsum(form, spec_real, weight_imag, preferred_element_type=jnp.float32)
    mixed_real = (mixed_real * keep_wide).astype(jnp.bfloat16) * doubling_low
    mixed_imag = (mixed_imag * keep_wide).astype(jnp.bfloat16) * doubling_low
    back_lines = inverse_cells(mixed_real, mixed_imag, cosines, sines)
    back_rows = lax.optimization_barrier(back_lines)
    skip_part = jnp.einsum(
        "oc,scxl->soxl", skip_weight, density_lines, preferred_element_type=jnp.float32
    )
    before = back_rows.astype(jnp.float32) + skip_part + skip_bias[None, :, None, None]
    gate_lines = (upstream_lines.astype(jnp.float32) * gelu_slope(before)).astype(jnp.bfloat16)
    grad_real, grad_imag = forward_parts(gate_lines, cosines, sines)
    scale = keep_wide * doubling
    grad_real = (grad_real * scale).astype(jnp.bfloat16)
    grad_imag = (grad_imag * scale).astype(jnp.bfloat16)
    outer = "slof,slcf->fco"
    part_real = jnp.einsum(
        outer, grad_real, spec_real, preferred_element_type=jnp.float32
    ) + jnp.einsum(outer, grad_imag, spec_imag, preferred_element_type=jnp.float32)
    part_imag = jnp.einsum(
        outer, grad_imag, spec_real, preferred_element_type=jnp.float32
    ) - jnp.einsum(outer, grad_real, spec_imag, preferred_element_type=jnp.float32)
    groups = lax.axis_size("dp")
    slabs = lax.axis_size("dom")
    rows_here = spectral_weight.shape[0]
    grad_local = jnp.stack([part_real, part_imag], 0).astype(jnp.bfloat16)
    grad_tiles = jnp.moveaxis(grad_local.reshape(groups, slabs, rows_here, channels), 1, 0)
    inner = "fco,slof->slcf"
    input_real = jnp.einsum(
        inner, weight_real, grad_real, preferred_element_type=jnp.float32
    ) + jnp.einsum(inner, weight_imag, grad_imag, preferred_element_type=jnp.float32)
    input_imag = jnp.einsum(
        inner, weight_real, grad_imag, preferred_element_type=jnp.float32
    ) - jnp.einsum(inner, weight_imag, grad_real, preferred_element_type=jnp.float32)
    input_lines = inverse_cells(
        input_real.astype(jnp.bfloat16), input_imag.astype(jnp.bfloat16), cosines, sines
    )
    input_rows = lax.optimization_barrier(input_lines)
    skip_back = jnp.einsum(
        "oc,soxl->scxl", skip_weight, gate_lines, preferred_element_type=jnp.float32
    )
    grad_lines = (input_rows.astype(jnp.float32) + skip_back).astype(jnp.bfloat16)
    group_grad = lax.all_to_all(grad_tiles, "dom", 0, 0, tiled=True)
    grad_lines, group_grad = lax.optimization_barrier((grad_lines, group_grad))
    input_grad = lax.all_to_all(grad_lines, "dom", split_axis=2, concat_axis=3, tiled=True)
    group_grad = group_grad.astype(jnp.float32).sum(axis=0)
    every_group = lax.all_gather(group_grad, "dp", axis=0, tiled=False)
    mine = lax.dynamic_index_in_dim(every_group, lax.axis_index("dp"), 1, keepdims=False)
    weight_grad = mine.sum(axis=0)
    new_moment_one = beta_first * moment_one + (1.0 - beta_first) * weight_grad
    new_moment_two = beta_second * moment_two + (1.0 - beta_second) * weight_grad * weight_grad
    first_hat = new_moment_one / (1.0 - beta_first**STEP)
    second_hat = new_moment_two / (1.0 - beta_second**STEP)
    new_weight = spectral_weight - learn_rate * (
        first_hat / (jnp.sqrt(second_hat) + epsilon) + decay_rate * spectral_weight
    )
    return lax.optimization_barrier((input_grad, new_weight, new_moment_one, new_moment_two))


def solution(mesh):
    placed = (
        P("dp", None, "dom", None),
        P("dp", None, "dom", None),
        P(("dp", "dom"), None),
        P(("dp", "dom"), None),
        P(("dp", "dom"), None),
        P(),
        P(),
        P(),
    )
    return jax.shard_map(
        on_device,
        mesh=mesh,
        in_specs=placed,
        out_specs=(
            P("dp", None, "dom", None),
            P(("dp", "dom"), None),
            P(("dp", "dom"), None),
            P(("dp", "dom"), None),
        ),
        check_vma=False,
    )
```

```python
import math

import jax
import jax.numpy as jnp
from jax import lax
from jax.sharding import PartitionSpec as P

MODES = 16
STEP = 10


learn_rate = 0.01
beta_first = 0.9
beta_second = 0.95
decay_rate = 0.1
epsilon = 1e-08


def joined_along(tiles, dim):
    dims = list(tiles.shape[1:])
    dims[dim] *= tiles.shape[0]
    return jnp.moveaxis(tiles, 0, dim).reshape(dims)


def copy_for_each(shard, axis):
    copies = jnp.broadcast_to(shard, (lax.axis_size(axis), *shard.shape))
    return lax.all_to_all(copies, axis, split_axis=0, concat_axis=0, tiled=True)


def collect(shard, axis, dim):
    return joined_along(copy_for_each(shard, axis), dim)


def in_one_piece(arrays, axis, split_dim, concat_dim, along):
    both = jnp.concatenate(arrays, axis=along)
    result, at, done = (
        lax.all_to_all(both, axis, split_axis=split_dim, concat_axis=concat_dim, tiled=True),
        0,
        [],
    )
    for a in arrays:
        done.append(lax.slice_in_dim(result, at, at + a.shape[along], axis=along))
        at += a.shape[along]
    return tuple(done)


def split_up(shard, dim, length):
    dims = shard.shape
    tiles = shard.reshape(*dims[:dim], length, dims[dim] // length, *dims[dim + 1 :])
    return jnp.moveaxis(tiles, dim, 0)


def sum_at_owner(shard, axis, dim):
    tiles = split_up(shard, dim, lax.axis_size(axis))
    arrived = lax.all_to_all(tiles, axis, split_axis=0, concat_axis=0, tiled=True)
    return arrived.astype(jnp.float32).sum(axis=0)


def summed_on_arrival(shard, axis, dim):
    length = lax.axis_size(axis)
    tiles = lax.all_to_all(split_up(shard, dim, length), axis, 0, 0, tiled=True)
    return jnp.sum(tiles, axis=0)


def axis_parts(count_xdim):
    freq_list = jnp.arange(MODES, dtype=jnp.int32)
    cell_list = jnp.arange(count_xdim, dtype=jnp.int32)
    phases = (
        jnp.mod(freq_list[:, None] * cell_list[None, :], count_xdim).astype(jnp.float32)
        / count_xdim
    )
    angles = 2.0 * math.pi * phases
    scaling = 1.0 / math.sqrt(count_xdim)
    return (
        (jnp.cos(angles) * scaling).astype(jnp.bfloat16),
        (jnp.sin(angles) * scaling).astype(jnp.bfloat16),
    )


def doubling_table():
    return jnp.where(jnp.arange(MODES, dtype=jnp.int32) > 0, 2.0, 1.0).astype(jnp.float32)


def gelu_slope(values):
    cumulative = 0.5 * (1.0 + lax.erf(values * 0.7071067811865476))
    bell_curve = jnp.exp(-0.5 * values * values) * 0.3989422804014327
    return cumulative + values * bell_curve


def forward_parts(field, cosines, sines):
    basis = jnp.concatenate([cosines, -sines], axis=0)
    both = jnp.einsum("scxl,gx->slcg", field, basis, preferred_element_type=jnp.float32)
    return (both[..., :MODES], both[..., MODES:])


def inverse_cells(values_real, values_imag, cosines, sines):
    basis = jnp.concatenate([cosines, -sines], axis=0)
    both = jnp.concatenate([values_real, values_imag], axis=3)
    return jnp.einsum("slcg,gx->scxl", both, basis, preferred_element_type=jnp.float32).astype(
        jnp.bfloat16
    )


def on_device(
    density, upstream, spectral_weight, moment_one, moment_two, skip_weight, skip_bias, mode_counts
):
    samples, channels, slab_rows, line_count = density.shape
    count_xdim = slab_rows * lax.axis_size("dom")
    cosines, sines = axis_parts(count_xdim)
    doubling = doubling_table()
    doubling_low = doubling.astype(jnp.bfloat16)
    counts_here = lax.dynamic_slice_in_dim(mode_counts, lax.axis_index("dp") * samples, samples, 0)
    keep_modes = (jnp.arange(MODES, dtype=jnp.int32)[None, :] < counts_here[:, None]).astype(
        jnp.float32
    )
    keep_wide = keep_modes[:, None, None, :]
    weight_short = spectral_weight.astype(jnp.bfloat16)
    rows_here = spectral_weight.shape[0]
    column_low = lax.all_gather(weight_short, "dp", axis=0, tiled=False)
    tile_shape = (channels, slab_rows, line_count // lax.axis_size("dom"))
    column_tiles = jnp.broadcast_to(
        column_low.reshape(channels, slab_rows, 1, tile_shape[2]),
        (channels, slab_rows, lax.axis_size("dom"), tile_shape[2]),
    ).reshape(density.shape)
    density_lines, upstream_lines, column_lines = in_one_piece(
        (density, upstream, column_tiles), "dom", 3, 2, 0
    )
    every_low = column_lines.reshape(channels, lax.axis_size("dom"), *tile_shape[1:])
    every_low = jnp.moveaxis(every_low, 1, 0).reshape(lax.axis_size("dom"), -1, rows_here, channels)
    weight_low = jnp.moveaxis(every_low, 0, 1).reshape(2, MODES, channels, channels)
    weight_real = weight_low[0]
    weight_imag = weight_low[1]
    real_part, imag_part = forward_parts(density_lines, cosines, sines)
    spec_real = real_part.astype(jnp.bfloat16)
    spec_imag = imag_part.astype(jnp.bfloat16)
    form = "slcf,fco->slof"
    mixed_real = jnp.einsum(
        form, spec_real, weight_real, preferred_element_type=jnp.float32
    ) - jnp.einsum(form, spec_imag, weight_imag, preferred_element_type=jnp.float32)
    mixed_imag = jnp.einsum(
        form, spec_imag, weight_real, preferred_element_type=jnp.float32
    ) + jnp.einsum(form, spec_real, weight_imag, preferred_element_type=jnp.float32)
    mixed_real = (mixed_real * keep_wide).astype(jnp.bfloat16) * doubling_low
    mixed_imag = (mixed_imag * keep_wide).astype(jnp.bfloat16) * doubling_low
    back_lines = inverse_cells(mixed_real, mixed_imag, cosines, sines)
    back_rows = lax.optimization_barrier(back_lines)
    skip_part = jnp.einsum(
        "oc,scxl->soxl", skip_weight, density_lines, preferred_element_type=jnp.float32
    )
    before = back_rows.astype(jnp.float32) + skip_part + skip_bias[None, :, None, None]
    gate_lines = (upstream_lines.astype(jnp.float32) * gelu_slope(before)).astype(jnp.bfloat16)
    grad_real, grad_imag = forward_parts(gate_lines, cosines, sines)
    scale = keep_wide * doubling
    grad_real = (grad_real * scale).astype(jnp.bfloat16)
    grad_imag = (grad_imag * scale).astype(jnp.bfloat16)
    outer = "slof,slcf->fco"
    part_real = jnp.einsum(
        outer, grad_real, spec_real, preferred_element_type=jnp.float32
    ) + jnp.einsum(outer, grad_imag, spec_imag, preferred_element_type=jnp.float32)
    part_imag = jnp.einsum(
        outer, grad_imag, spec_real, preferred_element_type=jnp.float32
    ) - jnp.einsum(outer, grad_real, spec_imag, preferred_element_type=jnp.float32)
    groups = lax.axis_size("dp")
    slabs = lax.axis_size("dom")
    rows_here = spectral_weight.shape[0]
    grad_local = jnp.stack([part_real, part_imag], 0).astype(jnp.bfloat16)
    grad_tiles = jnp.moveaxis(grad_local.reshape(groups, slabs, rows_here, channels), 1, 0)
    inner = "fco,slof->slcf"
    input_real = jnp.einsum(
        inner, weight_real, grad_real, preferred_element_type=jnp.float32
    ) + jnp.einsum(inner, weight_imag, grad_imag, preferred_element_type=jnp.float32)
    input_imag = jnp.einsum(
        inner, weight_real, grad_imag, preferred_element_type=jnp.float32
    ) - jnp.einsum(inner, weight_imag, grad_real, preferred_element_type=jnp.float32)
    input_lines = inverse_cells(
        input_real.astype(jnp.bfloat16), input_imag.astype(jnp.bfloat16), cosines, sines
    )
    input_rows = lax.optimization_barrier(input_lines)
    skip_back = jnp.einsum(
        "oc,soxl->scxl", skip_weight, gate_lines, preferred_element_type=jnp.float32
    )
    grad_lines = (input_rows.astype(jnp.float32) + skip_back).astype(jnp.bfloat16)
    owner_tiles = grad_local.reshape(groups * slabs, rows_here, channels)
    arrived = lax.all_to_all(owner_tiles, ("dp", "dom"), 0, 0, tiled=True)
    grad_lines, arrived = lax.optimization_barrier((grad_lines, arrived))
    input_grad = lax.all_to_all(grad_lines, "dom", split_axis=2, concat_axis=3, tiled=True)
    weight_grad = arrived.astype(jnp.float32).sum(axis=0)
    new_moment_one = beta_first * moment_one + (1.0 - beta_first) * weight_grad
    new_moment_two = beta_second * moment_two + (1.0 - beta_second) * weight_grad * weight_grad
    first_hat = new_moment_one / (1.0 - beta_first**STEP)
    second_hat = new_moment_two / (1.0 - beta_second**STEP)
    new_weight = spectral_weight - learn_rate * (
        first_hat / (jnp.sqrt(second_hat) + epsilon) + decay_rate * spectral_weight
    )
    return lax.optimization_barrier((input_grad, new_weight, new_moment_one, new_moment_two))


def solution(mesh):
    placed = (
        P("dp", None, "dom", None),
        P("dp", None, "dom", None),
        P(("dp", "dom"), None),
        P(("dp", "dom"), None),
        P(("dp", "dom"), None),
        P(),
        P(),
        P(),
    )
    return jax.shard_map(
        on_device,
        mesh=mesh,
        in_specs=placed,
        out_specs=(
            P("dp", None, "dom", None),
            P(("dp", "dom"), None),
            P(("dp", "dom"), None),
            P(("dp", "dom"), None),
        ),
        check_vma=False,
    )
```

```python
import math

import jax
import jax.numpy as jnp
from jax import lax
from jax.sharding import PartitionSpec as P

MODES = 16
STEP = 10


learn_rate = 0.01
beta_first = 0.9
beta_second = 0.95
decay_rate = 0.1
epsilon = 1e-08


def joined_along(tiles, dim):
    dims = list(tiles.shape[1:])
    dims[dim] *= tiles.shape[0]
    return jnp.moveaxis(tiles, 0, dim).reshape(dims)


def copy_for_each(shard, axis):
    copies = jnp.broadcast_to(shard, (lax.axis_size(axis), *shard.shape))
    return lax.all_to_all(copies, axis, split_axis=0, concat_axis=0, tiled=True)


def collect(shard, axis, dim):
    return joined_along(copy_for_each(shard, axis), dim)


def in_one_piece(arrays, axis, split_dim, concat_dim, along):
    both = jnp.concatenate(arrays, axis=along)
    result, at, done = (
        lax.all_to_all(both, axis, split_axis=split_dim, concat_axis=concat_dim, tiled=True),
        0,
        [],
    )
    for a in arrays:
        done.append(lax.slice_in_dim(result, at, at + a.shape[along], axis=along))
        at += a.shape[along]
    return tuple(done)


def split_up(shard, dim, length):
    dims = shard.shape
    tiles = shard.reshape(*dims[:dim], length, dims[dim] // length, *dims[dim + 1 :])
    return jnp.moveaxis(tiles, dim, 0)


def sum_at_owner(shard, axis, dim):
    tiles = split_up(shard, dim, lax.axis_size(axis))
    arrived = lax.all_to_all(tiles, axis, split_axis=0, concat_axis=0, tiled=True)
    return arrived.astype(jnp.float32).sum(axis=0)


def summed_on_arrival(shard, axis, dim):
    length = lax.axis_size(axis)
    tiles = lax.all_to_all(split_up(shard, dim, length), axis, 0, 0, tiled=True)
    return jnp.sum(tiles, axis=0)


def axis_parts(count_xdim):
    freq_list = jnp.arange(MODES, dtype=jnp.int32)
    cell_list = jnp.arange(count_xdim, dtype=jnp.int32)
    phases = (
        jnp.mod(freq_list[:, None] * cell_list[None, :], count_xdim).astype(jnp.float32)
        / count_xdim
    )
    angles = 2.0 * math.pi * phases
    scaling = 1.0 / math.sqrt(count_xdim)
    return (
        (jnp.cos(angles) * scaling).astype(jnp.bfloat16),
        (jnp.sin(angles) * scaling).astype(jnp.bfloat16),
    )


def doubling_table():
    return jnp.where(jnp.arange(MODES, dtype=jnp.int32) > 0, 2.0, 1.0).astype(jnp.float32)


def gelu_slope(values):
    cumulative = 0.5 * (1.0 + lax.erf(values * 0.7071067811865476))
    bell_curve = jnp.exp(-0.5 * values * values) * 0.3989422804014327
    return cumulative + values * bell_curve


def forward_parts(field, cosines, sines):
    basis = jnp.concatenate([cosines, -sines], axis=0)
    both = jnp.einsum("scxl,gx->slcg", field, basis, preferred_element_type=jnp.float32)
    return (both[..., :MODES], both[..., MODES:])


def inverse_cells(values_real, values_imag, cosines, sines):
    basis = jnp.concatenate([cosines, -sines], axis=0)
    both = jnp.concatenate([values_real, values_imag], axis=3)
    return jnp.einsum("slcg,gx->scxl", both, basis, preferred_element_type=jnp.float32).astype(
        jnp.bfloat16
    )


def on_device(
    density, upstream, spectral_weight, moment_one, moment_two, skip_weight, skip_bias, mode_counts
):
    samples, channels, slab_rows, line_count = density.shape
    count_xdim = slab_rows * lax.axis_size("dom")
    cosines, sines = axis_parts(count_xdim)
    doubling = doubling_table()
    doubling_low = doubling.astype(jnp.bfloat16)
    counts_here = lax.dynamic_slice_in_dim(mode_counts, lax.axis_index("dp") * samples, samples, 0)
    keep_modes = (jnp.arange(MODES, dtype=jnp.int32)[None, :] < counts_here[:, None]).astype(
        jnp.float32
    )
    keep_wide = keep_modes[:, None, None, :]
    weight_short = spectral_weight.astype(jnp.bfloat16)
    rows_here = spectral_weight.shape[0]
    column_low = lax.all_gather(weight_short, "dp", axis=0, tiled=False)
    tile_shape = (channels, slab_rows, line_count // lax.axis_size("dom"))
    column_tiles = jnp.broadcast_to(
        column_low.reshape(channels, slab_rows, 1, tile_shape[2]),
        (channels, slab_rows, lax.axis_size("dom"), tile_shape[2]),
    ).reshape(density.shape)
    density_lines, upstream_lines, column_lines = in_one_piece(
        (density, upstream, column_tiles), "dom", 3, 2, 0
    )
    every_low = column_lines.reshape(channels, lax.axis_size("dom"), *tile_shape[1:])
    every_low = jnp.moveaxis(every_low, 1, 0).reshape(lax.axis_size("dom"), -1, rows_here, channels)
    weight_low = jnp.moveaxis(every_low, 0, 1).reshape(2, MODES, channels, channels)
    weight_real = weight_low[0]
    weight_imag = weight_low[1]
    real_part, imag_part = forward_parts(density_lines, cosines, sines)
    spec_real = real_part.astype(jnp.bfloat16)
    spec_imag = imag_part.astype(jnp.bfloat16)
    form = "slcf,fco->slof"
    mixed_real = jnp.einsum(
        form, spec_real, weight_real, preferred_element_type=jnp.float32
    ) - jnp.einsum(form, spec_imag, weight_imag, preferred_element_type=jnp.float32)
    mixed_imag = jnp.einsum(
        form, spec_imag, weight_real, preferred_element_type=jnp.float32
    ) + jnp.einsum(form, spec_real, weight_imag, preferred_element_type=jnp.float32)
    mixed_real = (mixed_real * keep_wide).astype(jnp.bfloat16) * doubling_low
    mixed_imag = (mixed_imag * keep_wide).astype(jnp.bfloat16) * doubling_low
    back_lines = inverse_cells(mixed_real, mixed_imag, cosines, sines)
    back_rows = lax.optimization_barrier(back_lines)
    skip_part = jnp.einsum(
        "oc,scxl->soxl", skip_weight, density_lines, preferred_element_type=jnp.float32
    )
    before = back_rows.astype(jnp.float32) + skip_part + skip_bias[None, :, None, None]
    gate_lines = (upstream_lines.astype(jnp.float32) * gelu_slope(before)).astype(jnp.bfloat16)
    grad_real, grad_imag = forward_parts(gate_lines, cosines, sines)
    scale = keep_wide * doubling
    grad_real = (grad_real * scale).astype(jnp.bfloat16)
    grad_imag = (grad_imag * scale).astype(jnp.bfloat16)
    outer = "slof,slcf->fco"
    part_real = jnp.einsum(
        outer, grad_real, spec_real, preferred_element_type=jnp.float32
    ) + jnp.einsum(outer, grad_imag, spec_imag, preferred_element_type=jnp.float32)
    part_imag = jnp.einsum(
        outer, grad_imag, spec_real, preferred_element_type=jnp.float32
    ) - jnp.einsum(outer, grad_real, spec_imag, preferred_element_type=jnp.float32)
    groups = lax.axis_size("dp")
    slabs = lax.axis_size("dom")
    rows_here = spectral_weight.shape[0]
    grad_local = jnp.stack([part_real, part_imag], 0).astype(jnp.bfloat16)
    grad_tiles = jnp.moveaxis(grad_local.reshape(groups, slabs, rows_here, channels), 1, 0)
    inner = "fco,slof->slcf"
    input_real = jnp.einsum(
        inner, weight_real, grad_real, preferred_element_type=jnp.float32
    ) + jnp.einsum(inner, weight_imag, grad_imag, preferred_element_type=jnp.float32)
    input_imag = jnp.einsum(
        inner, weight_real, grad_imag, preferred_element_type=jnp.float32
    ) - jnp.einsum(inner, weight_imag, grad_real, preferred_element_type=jnp.float32)
    input_lines = inverse_cells(
        input_real.astype(jnp.bfloat16), input_imag.astype(jnp.bfloat16), cosines, sines
    )
    input_rows = lax.optimization_barrier(input_lines)
    skip_back = jnp.einsum(
        "oc,soxl->scxl", skip_weight, gate_lines, preferred_element_type=jnp.float32
    )
    grad_lines = (input_rows.astype(jnp.float32) + skip_back).astype(jnp.bfloat16)
    group_grad = lax.all_to_all(grad_tiles, "dom", 0, 0, tiled=True)
    lines_here = grad_lines.shape[3]
    line_tiles = grad_lines.reshape(samples, channels, slabs, slab_rows, lines_here)
    line_tiles = jnp.moveaxis(line_tiles, 2, 0)
    line_tiles, group_grad = lax.optimization_barrier((line_tiles, group_grad))
    input_grad = lax.all_to_all(line_tiles, "dom", 0, 0, tiled=True)
    input_grad = jnp.moveaxis(input_grad, 0, 3).reshape(samples, channels, slab_rows, -1)
    group_grad = group_grad.astype(jnp.float32).sum(axis=0)
    every_group = lax.all_gather(group_grad, "dp", axis=0, tiled=False)
    mine = lax.dynamic_index_in_dim(every_group, lax.axis_index("dp"), 1, keepdims=False)
    weight_grad = mine.sum(axis=0)
    new_moment_one = beta_first * moment_one + (1.0 - beta_first) * weight_grad
    new_moment_two = beta_second * moment_two + (1.0 - beta_second) * weight_grad * weight_grad
    first_hat = new_moment_one / (1.0 - beta_first**STEP)
    second_hat = new_moment_two / (1.0 - beta_second**STEP)
    new_weight = spectral_weight - learn_rate * (
        first_hat / (jnp.sqrt(second_hat) + epsilon) + decay_rate * spectral_weight
    )
    return lax.optimization_barrier((input_grad, new_weight, new_moment_one, new_moment_two))


def solution(mesh):
    placed = (
        P("dp", None, "dom", None),
        P("dp", None, "dom", None),
        P(("dp", "dom"), None),
        P(("dp", "dom"), None),
        P(("dp", "dom"), None),
        P(),
        P(),
        P(),
    )
    return jax.shard_map(
        on_device,
        mesh=mesh,
        in_specs=placed,
        out_specs=(
            P("dp", None, "dom", None),
            P(("dp", "dom"), None),
            P(("dp", "dom"), None),
            P(("dp", "dom"), None),
        ),
        check_vma=False,
    )
```

```python
import math

import jax
import jax.numpy as jnp
from jax import lax
from jax.sharding import PartitionSpec as P

MODES = 16
STEP = 10


learn_rate = 0.01
beta_first = 0.9
beta_second = 0.95
decay_rate = 0.1
epsilon = 1e-08


def joined_along(tiles, dim):
    dims = list(tiles.shape[1:])
    dims[dim] *= tiles.shape[0]
    return jnp.moveaxis(tiles, 0, dim).reshape(dims)


def copy_for_each(shard, axis):
    copies = jnp.broadcast_to(shard, (lax.axis_size(axis), *shard.shape))
    return lax.all_to_all(copies, axis, split_axis=0, concat_axis=0, tiled=True)


def collect(shard, axis, dim):
    return joined_along(copy_for_each(shard, axis), dim)


def in_one_piece(arrays, axis, split_dim, concat_dim, along):
    both = jnp.concatenate(arrays, axis=along)
    result, at, done = (
        lax.all_to_all(both, axis, split_axis=split_dim, concat_axis=concat_dim, tiled=True),
        0,
        [],
    )
    for a in arrays:
        done.append(lax.slice_in_dim(result, at, at + a.shape[along], axis=along))
        at += a.shape[along]
    return tuple(done)


def split_up(shard, dim, length):
    dims = shard.shape
    tiles = shard.reshape(*dims[:dim], length, dims[dim] // length, *dims[dim + 1 :])
    return jnp.moveaxis(tiles, dim, 0)


def sum_at_owner(shard, axis, dim):
    tiles = split_up(shard, dim, lax.axis_size(axis))
    arrived = lax.all_to_all(tiles, axis, split_axis=0, concat_axis=0, tiled=True)
    return arrived.astype(jnp.float32).sum(axis=0)


def summed_on_arrival(shard, axis, dim):
    length = lax.axis_size(axis)
    tiles = lax.all_to_all(split_up(shard, dim, length), axis, 0, 0, tiled=True)
    return jnp.sum(tiles, axis=0)


def axis_parts(count_xdim):
    freq_list = jnp.arange(MODES, dtype=jnp.int32)
    cell_list = jnp.arange(count_xdim, dtype=jnp.int32)
    phases = (
        jnp.mod(freq_list[:, None] * cell_list[None, :], count_xdim).astype(jnp.float32)
        / count_xdim
    )
    angles = 2.0 * math.pi * phases
    scaling = 1.0 / math.sqrt(count_xdim)
    return (
        (jnp.cos(angles) * scaling).astype(jnp.bfloat16),
        (jnp.sin(angles) * scaling).astype(jnp.bfloat16),
    )


def doubling_table():
    return jnp.where(jnp.arange(MODES, dtype=jnp.int32) > 0, 2.0, 1.0).astype(jnp.float32)


def gelu_slope(values):
    cumulative = 0.5 * (1.0 + lax.erf(values * 0.7071067811865476))
    bell_curve = jnp.exp(-0.5 * values * values) * 0.3989422804014327
    return cumulative + values * bell_curve


def forward_parts(field, cosines, sines):
    basis = jnp.concatenate([cosines, -sines], axis=0)
    both = jnp.einsum("scxl,gx->slcg", field, basis, preferred_element_type=jnp.float32)
    return (both[..., :MODES], both[..., MODES:])


def inverse_cells(values_real, values_imag, cosines, sines):
    basis = jnp.concatenate([cosines, -sines], axis=0)
    both = jnp.concatenate([values_real, values_imag], axis=3)
    return jnp.einsum("slcg,gx->scxl", both, basis, preferred_element_type=jnp.float32).astype(
        jnp.bfloat16
    )


def on_device(
    density, upstream, spectral_weight, moment_one, moment_two, skip_weight, skip_bias, mode_counts
):
    samples, channels, slab_rows, line_count = density.shape
    count_xdim = slab_rows * lax.axis_size("dom")
    cosines, sines = axis_parts(count_xdim)
    doubling = doubling_table()
    doubling_low = doubling.astype(jnp.bfloat16)
    counts_here = lax.dynamic_slice_in_dim(mode_counts, lax.axis_index("dp") * samples, samples, 0)
    keep_modes = (jnp.arange(MODES, dtype=jnp.int32)[None, :] < counts_here[:, None]).astype(
        jnp.float32
    )
    keep_wide = keep_modes[:, None, None, :]
    weight_short = spectral_weight.astype(jnp.bfloat16)
    rows_here = spectral_weight.shape[0]
    column_low = lax.all_gather(weight_short, "dp", axis=0, tiled=False)
    tile_shape = (channels, slab_rows, line_count // lax.axis_size("dom"))
    column_tiles = jnp.broadcast_to(
        column_low.reshape(channels, slab_rows, 1, tile_shape[2]),
        (channels, slab_rows, lax.axis_size("dom"), tile_shape[2]),
    ).reshape(density.shape)
    density_lines, upstream_lines, column_lines = in_one_piece(
        (density, upstream, column_tiles), "dom", 3, 2, 0
    )
    every_low = column_lines.reshape(channels, lax.axis_size("dom"), *tile_shape[1:])
    every_low = jnp.moveaxis(every_low, 1, 0).reshape(lax.axis_size("dom"), -1, rows_here, channels)
    weight_low = jnp.moveaxis(every_low, 0, 1).reshape(2, MODES, channels, channels)
    weight_real = weight_low[0]
    weight_imag = weight_low[1]
    real_part, imag_part = forward_parts(density_lines, cosines, sines)
    spec_real = real_part.astype(jnp.bfloat16)
    spec_imag = imag_part.astype(jnp.bfloat16)
    form = "slcf,fco->slof"
    mixed_real = jnp.einsum(
        form, spec_real, weight_real, preferred_element_type=jnp.float32
    ) - jnp.einsum(form, spec_imag, weight_imag, preferred_element_type=jnp.float32)
    mixed_imag = jnp.einsum(
        form, spec_imag, weight_real, preferred_element_type=jnp.float32
    ) + jnp.einsum(form, spec_real, weight_imag, preferred_element_type=jnp.float32)
    mixed_real = (mixed_real * keep_wide).astype(jnp.bfloat16) * doubling_low
    mixed_imag = (mixed_imag * keep_wide).astype(jnp.bfloat16) * doubling_low
    back_lines = inverse_cells(mixed_real, mixed_imag, cosines, sines)
    back_rows = lax.optimization_barrier(back_lines)
    skip_part = jnp.einsum(
        "oc,scxl->soxl", skip_weight, density_lines, preferred_element_type=jnp.float32
    )
    before = back_rows.astype(jnp.float32) + skip_part + skip_bias[None, :, None, None]
    gate_lines = (upstream_lines.astype(jnp.float32) * gelu_slope(before)).astype(jnp.bfloat16)
    grad_real, grad_imag = forward_parts(gate_lines, cosines, sines)
    scale = keep_wide * doubling
    grad_real = (grad_real * scale).astype(jnp.bfloat16)
    grad_imag = (grad_imag * scale).astype(jnp.bfloat16)
    outer = "slof,slcf->fco"
    part_real = jnp.einsum(
        outer, grad_real, spec_real, preferred_element_type=jnp.float32
    ) + jnp.einsum(outer, grad_imag, spec_imag, preferred_element_type=jnp.float32)
    part_imag = jnp.einsum(
        outer, grad_imag, spec_real, preferred_element_type=jnp.float32
    ) - jnp.einsum(outer, grad_real, spec_imag, preferred_element_type=jnp.float32)
    groups = lax.axis_size("dp")
    slabs = lax.axis_size("dom")
    rows_here = spectral_weight.shape[0]
    grad_local = jnp.stack([part_real, part_imag], 0).astype(jnp.bfloat16)
    grad_tiles = jnp.moveaxis(grad_local.reshape(groups, slabs, rows_here, channels), 1, 0)
    inner = "fco,slof->slcf"
    input_real = jnp.einsum(
        inner, weight_real, grad_real, preferred_element_type=jnp.float32
    ) + jnp.einsum(inner, weight_imag, grad_imag, preferred_element_type=jnp.float32)
    input_imag = jnp.einsum(
        inner, weight_real, grad_imag, preferred_element_type=jnp.float32
    ) - jnp.einsum(inner, weight_imag, grad_real, preferred_element_type=jnp.float32)
    input_lines = inverse_cells(
        input_real.astype(jnp.bfloat16), input_imag.astype(jnp.bfloat16), cosines, sines
    )
    input_rows = lax.optimization_barrier(input_lines)
    skip_back = jnp.einsum(
        "oc,soxl->scxl", skip_weight, gate_lines, preferred_element_type=jnp.float32
    )
    grad_lines = (input_rows.astype(jnp.float32) + skip_back).astype(jnp.bfloat16)
    group_grad = lax.all_to_all(grad_tiles, "dom", 0, 0, tiled=True)
    grad_lines, group_grad = lax.optimization_barrier((grad_lines, group_grad))
    input_grad = lax.all_to_all(grad_lines, "dom", split_axis=2, concat_axis=3, tiled=True)
    group_grad = group_grad.astype(jnp.float32).sum(axis=0)
    every_group = lax.all_gather(group_grad.astype(jnp.bfloat16), "dp", axis=0, tiled=False)
    mine = lax.dynamic_index_in_dim(every_group, lax.axis_index("dp"), 1, keepdims=False)
    weight_grad = mine.astype(jnp.float32).sum(axis=0)
    new_moment_one = beta_first * moment_one + (1.0 - beta_first) * weight_grad
    new_moment_two = beta_second * moment_two + (1.0 - beta_second) * weight_grad * weight_grad
    first_hat = new_moment_one / (1.0 - beta_first**STEP)
    second_hat = new_moment_two / (1.0 - beta_second**STEP)
    new_weight = spectral_weight - learn_rate * (
        first_hat / (jnp.sqrt(second_hat) + epsilon) + decay_rate * spectral_weight
    )
    return lax.optimization_barrier((input_grad, new_weight, new_moment_one, new_moment_two))


def solution(mesh):
    placed = (
        P("dp", None, "dom", None),
        P("dp", None, "dom", None),
        P(("dp", "dom"), None),
        P(("dp", "dom"), None),
        P(("dp", "dom"), None),
        P(),
        P(),
        P(),
    )
    return jax.shard_map(
        on_device,
        mesh=mesh,
        in_specs=placed,
        out_specs=(
            P("dp", None, "dom", None),
            P(("dp", "dom"), None),
            P(("dp", "dom"), None),
            P(("dp", "dom"), None),
        ),
        check_vma=False,
    )
```
